128 devices in a mesh: inline: 16 (over z, x), crosslin: 8 (over y, core).
Axes of the slice: x: 4, y: 4, z: 4, core: 2. Of those that a mesh axis runs over, the one named last changes fastest.
Arguments:
- grid_feat: bfloat16 [262144, 512], P(('inline', 'crosslin')), may hold values from -68 to 68
- cotangent: bfloat16 [262144, 512], P(('inline', 'crosslin')), may hold values from -6 to 6
- trace_feat: bfloat16 [16384, 512], P(('inline', 'crosslin')), may hold values from -6 to 6
- trace_dest: int32 [16384, 2], P(('inline', 'crosslin')), may hold values from 0 to 127, all different within a row; in each aligned block of 128 rows (0 to 127, 128 to 255, ...) at most 4 rows name the same one
- query_weight: bfloat16 [512, 512], replicated, may hold values from -0.25 to 0.25
- key_weight: bfloat16 [512, 512], replicated, may hold values from -0.25 to 0.25
- value_weight: bfloat16 [512, 512], replicated, may hold values from -0.25 to 0.25
- output_weight: bfloat16 [512, 512], replicated, may hold values from -0.25 to 0.25
Outputs:
- grad_grid: bfloat16 [262144, 512], P(('inline', 'crosslin'))
- grad_trace: float32 [16384, 512], P(('inline', 'crosslin'))
- grad_query: float32 [512, 512], replicated
- grad_key: float32 [512, 512], replicated
- grad_value: float32 [512, 512], replicated
- grad_output: float32 [512, 512], replicated
The draws below stay inside these ranges and needn't reach their ends.
Inputs may be any that keep to these rules, and one draw needn't show every extreme that they name: `trace_dest`: in the 128 rows of one device no tile is named by more than 4 rows, a bound that some block reaches; a row names 2 different tiles; every tile is named by some row.
All inputs are finite; a program needn't handle non-finite values.
Results may differ from the reference program's by a relative error of at most 0.013.
The reference program's roundings to bfloat16 on the way count: a program that leaves them out, or rounds other values in their place, can miss the bound.
Values may be sent and summed in bfloat16 or wider, within the bound.
No kernel may reach another device: no remote copies, remote signals or barrier semaphores. Data moves between devices by JAX's collectives and lax.ppermute only.
A program may use at most 64 MiB of HBM per device.

```python
import math
import jax
import jax.numpy as jnp
import numpy as np
from jax import lax

D = 512
HEADS = 8
TOP = 2
GQ = 2048
TR_DEV = 128
TILES = 128
CAP = 4
SLOTS = 512
GRID = 262144
TRACES = 16384


def draw_grid_feat(key, part):
    first = jax.random.fold_in(key, 0)
    values = jnp.clip(jax.random.normal(first, (GRID, D), jnp.float32), -6.0, 6.0)
    return values.astype(jnp.bfloat16)


def block_levels(key, shape, cuts, least, largest):
    def one(axis_at, parts):
        heights = jax.random.uniform(jax.random.fold_in(jax.random.fold_in(key, 6), axis_at), (parts,), jnp.float32, least / len(cuts), largest / len(cuts))
        return jnp.repeat(jnp.exp(heights), shape[axis_at] // parts).reshape((-1,) + (1,) * (len(shape) - axis_at - 1))

    factor_of = one(*cuts[0])
    for cut in cuts[1:]:
        factor_of = factor_of * one(*cut)
    return factor_of


def deal_out(key, own, number, rows, number_of, top, bound, lean):
    order = jax.random.permutation(key, number_of)
    crowded, usual = load_shares(number_of, rows * top, bound, lean, True), load_shares(number_of, rows * top, bound, lean, False)
    places = jnp.arange(number_of)

    def named(lengths, offset_by):
        used = int((lengths > 0).sum())
        fixed = max(1, used // 4)
        shifted = fixed + (places - fixed + offset_by * (used - fixed)) % max(1, number_of - fixed)
        return jnp.zeros((number_of,), jnp.int32).at[order[jnp.where(places < fixed, places, shifted)]].set(jnp.asarray(lengths, jnp.int32))

    lengths = jnp.where(number % 4 == 0, named(crowded, number // 4), named(usual, number - number // 4 - 1))
    mixed = jax.random.permutation(jax.random.fold_in(own, 3), number_of)
    source_of, sink = mixed[0:number_of // 2 * 2:2], mixed[1:number_of // 2 * 2:2]
    margin = jnp.minimum(lengths[source_of] - 1, bound - lengths[sink]) // 2
    margin = jnp.where((source_of == order[0]) | (sink == order[0]) | (lengths[sink] == 0), 0, jnp.maximum(margin, 0))
    shifted = jax.random.randint(jax.random.fold_in(own, 4), (number_of // 2,), 0, 1 << 20) % (margin + 1)
    lengths = lengths.at[source_of].add(-shifted).at[sink].add(shifted)
    members = jnp.searchsorted(jnp.cumsum(lengths), jnp.arange(rows * top), side="right").astype(jnp.int32)
    listing = members.reshape(top, rows).T
    listing = listing[jax.random.permutation(jax.random.fold_in(own, 1), rows)]
    offset_by = jax.random.randint(jax.random.fold_in(own, 2), (rows, 1), 0, top)
    return jnp.take_along_axis(listing, (jnp.arange(top)[None, :] + offset_by) % top, axis=1)


def load_shares(number_of, total, bound, skew, full):
    loads = [(1 << 20) // math.isqrt(grade ** skew) + 1 for grade in range(1, number_of + 1)]
    largest = bound if full else min(bound, max(-(-total // number_of), total * loads[0] // sum(loads)))
    least = 1 if total - largest >= number_of - 1 else 0
    given, surplus = [largest] + [least] * (number_of - 1), total - largest - least * (number_of - 1)
    while surplus > 0:
        free = [i for i in range(1, number_of) if given[i] < largest] or [i for i in range(1, number_of) if given[i] < bound]
        pool, budget = sum([loads[i] for i in free]), surplus
        for i in free:
            addition = min(bound - given[i], max(1, budget * loads[i] // pool), surplus)
            given[i] = given[i] + addition
            surplus = surplus - addition
    return np.array(given)


def scatter_about(key, dims, scale, most, cuts=(), kind=jnp.bfloat16):
    result = jax.random.normal(key, dims, jnp.float32) * scale
    if len(cuts) > 0:
        result = block_levels(key, dims, cuts, -0.22, 0.18) * result
    return jnp.clip(result, min=-most, max=most).astype(kind)


def setup_inputs(seed: int = 0) -> dict:
    splits = jax.random.split(jax.random.key(seed), 9)
    grid_feat = draw_grid_feat(jax.random.fold_in(splits[8], 71), 0)
    cotangent = scatter_about(splits[1], (GRID, D), 1.0, 6.0, ((0, 128),))
    trace_feat = scatter_about(splits[2], (TRACES, D), 1.0, 6.0, ((0, 128),))
    trace_dest_keys = jax.random.split(jax.random.fold_in(splits[3], 1), TRACES // TR_DEV)
    trace_dest_turns = jax.random.permutation(jax.random.fold_in(splits[3], 3), TRACES // TR_DEV)
    trace_dest = jax.vmap(lambda own, number: deal_out(jax.random.fold_in(splits[3], 2), own, number, TR_DEV, TILES, TOP, CAP, 2))(trace_dest_keys, trace_dest_turns).reshape((TRACES, TOP))
    query_weight = scatter_about(splits[4], (D, D), D ** -0.5, 0.25)
    key_weight = scatter_about(splits[5], (D, D), D ** -0.5, 0.25)
    value_weight = scatter_about(splits[6], (D, D), D ** -0.5, 0.25)
    output_weight = scatter_about(splits[7], (D, D), D ** -0.5, 0.25)
    return dict(grid_feat=grid_feat, cotangent=cotangent, trace_feat=trace_feat, trace_dest=trace_dest, query_weight=query_weight, key_weight=key_weight, value_weight=value_weight, output_weight=output_weight)


def slot_table(targets, tile_count, capacity):
    tile_ids = jnp.arange(tile_count, dtype=jnp.int32)
    named = jnp.any(targets[:, :, None] == tile_ids[None, None, :], axis=1)
    position = jnp.cumsum(named.astype(jnp.int32), axis=0) - 1
    places = jnp.arange(capacity, dtype=jnp.int32)
    chosen = named.T[:, None, :] & (position.T[:, None, :] == places[None, :, None])
    return (chosen, lax.optimization_barrier(jnp.sum(named.astype(jnp.int32), axis=0)))

def tile_grad(grid_rows, upstream, query_weight, output_weight, key_tile, value_tile, live_slots):
    model_width = grid_rows.shape[1]
    head_size = model_width // HEADS
    factor = head_size ** (-0.5)
    queries = jnp.dot(grid_rows, query_weight, preferred_element_type=jnp.float32).astype(jnp.bfloat16)
    out_grad = jnp.dot(upstream, output_weight.T, preferred_element_type=jnp.float32).astype(jnp.bfloat16)

    def one_head(head_index):
        offset = head_index * head_size
        query_head = lax.dynamic_slice_in_dim(queries, offset, head_size, 1)
        key_head = lax.dynamic_slice_in_dim(key_tile, offset, head_size, 1)
        value_head = lax.dynamic_slice_in_dim(value_tile, offset, head_size, 1)
        grad_head = lax.dynamic_slice_in_dim(out_grad, offset, head_size, 1)
        scores = jnp.dot(query_head, key_head.T, preferred_element_type=jnp.float32) * factor
        scores = jnp.where(live_slots[None, :], scores, -1e+30)
        row_peak = lax.optimization_barrier(jnp.max(scores, axis=1, keepdims=True))
        raised = jnp.exp(scores - row_peak)
        attention = raised / lax.optimization_barrier(jnp.sum(raised, axis=1, keepdims=True))
        prob_half = attention.astype(jnp.bfloat16)
        head_out = jnp.dot(prob_half, value_head, preferred_element_type=jnp.float32).astype(jnp.bfloat16)
        prob_grad = jnp.dot(grad_head, value_head.T, preferred_element_type=jnp.float32)
        correction = lax.optimization_barrier(jnp.sum(attention * prob_grad, axis=1, keepdims=True))
        score_grad = (attention * (prob_grad - correction) * factor).astype(jnp.bfloat16)
        query_grad = jnp.dot(score_grad, key_head, preferred_element_type=jnp.float32).astype(jnp.bfloat16)
        key_grad = jnp.dot(score_grad.T, query_head, preferred_element_type=jnp.float32).astype(jnp.bfloat16)
        value_grad = jnp.dot(prob_half.T, grad_head, preferred_element_type=jnp.float32).astype(jnp.bfloat16)
        return (head_out, query_grad, key_grad, value_grad)

    def join_heads(stacked):
        return jnp.transpose(stacked, (1, 0, 2)).reshape(stacked.shape[1], model_width)
    stacked = lax.map(one_head, jnp.arange(HEADS, dtype=jnp.int32))
    attn_out, query_grad, key_grad, value_grad = [join_heads(stacked_part) for stacked_part in stacked]
    part_output = jnp.dot(attn_out.T, upstream, preferred_element_type=jnp.float32)
    grad_grid = jnp.dot(query_grad, query_weight.T, preferred_element_type=jnp.float32).astype(jnp.bfloat16)
    part_query = jnp.dot(grid_rows.T, query_grad, preferred_element_type=jnp.float32)
    return (grad_grid, key_grad, value_grad, part_output, part_query)

def reference(grid_feat, cotangent, trace_feat, trace_dest, query_weight, key_weight, value_weight, output_weight):
    blocks = trace_dest.reshape(TILES, TR_DEV, TOP)
    row_ids = jnp.arange(TR_DEV, dtype=jnp.int32)

    def block_slots(targets):
        chosen, counts = slot_table(targets, TILES, CAP)
        local_index = lax.optimization_barrier(jnp.sum(jnp.where(chosen, row_ids[None, None, :], 0), axis=2)).astype(jnp.int32)
        return (local_index, jnp.any(chosen, axis=2))
    local_index, filled = lax.map(block_slots, blocks)
    slot_rows = local_index + (jnp.arange(TILES, dtype=jnp.int32) * TR_DEV)[:, None, None]
    slot_rows = jnp.transpose(slot_rows, (1, 0, 2)).reshape(TILES, SLOTS).astype(jnp.int32)
    filled = jnp.transpose(filled, (1, 0, 2)).reshape(TILES, SLOTS)
    key_rows = jnp.dot(trace_feat, key_weight, preferred_element_type=jnp.float32).astype(jnp.bfloat16)
    value_rows = jnp.dot(trace_feat, value_weight, preferred_element_type=jnp.float32).astype(jnp.bfloat16)
    grid_tiles = grid_feat.reshape(TILES, GQ, D)
    upstream_tiles = cotangent.reshape(TILES, GQ, D)

    def one_tile(totals, tile_inputs):
        grid_rows, upstream, rows_here, live_slots = tile_inputs
        key_tile = jnp.take(key_rows, rows_here, axis=0)
        value_tile = jnp.take(value_rows, rows_here, axis=0)
        grad_grid, key_grad, value_grad, part_output, part_query = tile_grad(grid_rows, upstream, query_weight, output_weight, key_tile, value_tile, live_slots)
        slot_trace = jnp.dot(key_grad, key_weight.T, preferred_element_type=jnp.float32)
        slot_trace = (slot_trace + jnp.dot(value_grad, value_weight.T, preferred_element_type=jnp.float32)).astype(jnp.bfloat16)
        return ((totals[0] + part_output, totals[1] + part_query), (grad_grid, key_grad, value_grad, slot_trace))
    zeroed = jnp.zeros((D, D), jnp.float32)
    (grad_output, grad_query), (grad_grid, key_grads, value_grads, slot_traces) = lax.scan(one_tile, (zeroed, zeroed), (grid_tiles, upstream_tiles, slot_rows, filled))
    flat_rows = slot_rows.reshape(-1)
    key_sum = jnp.zeros((TRACES, D), jnp.float32).at[flat_rows].add(key_grads.reshape(-1, D).astype(jnp.float32))
    value_sum = jnp.zeros((TRACES, D), jnp.float32).at[flat_rows].add(value_grads.reshape(-1, D).astype(jnp.float32))
    grad_trace = jnp.zeros((TRACES, D), jnp.float32).at[flat_rows].add(slot_traces.reshape(-1, D).astype(jnp.float32))
    trace_wide = trace_feat.astype(jnp.float32)
    grad_key = jnp.dot(trace_wide.T, key_sum, precision=lax.Precision.HIGHEST)
    grad_value = jnp.dot(trace_wide.T, value_sum, precision=lax.Precision.HIGHEST)
    return (grad_grid.reshape(GRID, D), grad_trace, grad_query, grad_key, grad_value, grad_output)
```

```python
import jax
import jax.numpy as jnp
from jax import lax
from jax.sharding import PartitionSpec as P

HEADS = 8
TOP = 2


def slot_table(targets, tile_count, capacity):
    tile_ids = jnp.arange(tile_count, dtype=jnp.int32)
    named = jnp.any(targets[:, :, None] == tile_ids[None, None, :], axis=1)
    position = jnp.cumsum(named.astype(jnp.int32), axis=0) - 1
    places = jnp.arange(capacity, dtype=jnp.int32)
    chosen = named.T[:, None, :] & (position.T[:, None, :] == places[None, :, None])
    return (chosen, jnp.sum(named.astype(jnp.int32), axis=0))


def tile_grad(grid_rows, upstream, query_weight, output_weight, key_tile, value_tile, live_slots):
    model_width = grid_rows.shape[1]
    head_size = model_width // HEADS
    factor = head_size ** (-0.5)
    queries = jnp.dot(grid_rows, query_weight, preferred_element_type=jnp.float32).astype(
        jnp.bfloat16
    )
    out_grad = jnp.dot(upstream, output_weight.T, preferred_element_type=jnp.float32).astype(
        jnp.bfloat16
    )

    def one_head(head_index):
        offset = head_index * head_size
        query_head = lax.dynamic_slice_in_dim(queries, offset, head_size, 1)
        key_head = lax.dynamic_slice_in_dim(key_tile, offset, head_size, 1)
        value_head = lax.dynamic_slice_in_dim(value_tile, offset, head_size, 1)
        grad_head = lax.dynamic_slice_in_dim(out_grad, offset, head_size, 1)
        scores = jnp.dot(query_head, key_head.T, preferred_element_type=jnp.float32) * factor
        scores = jnp.where(live_slots[None, :], scores, -1e30)
        row_peak = jnp.max(scores, axis=1, keepdims=True)
        raised = jnp.exp(scores - row_peak)
        attention = raised / jnp.sum(raised, axis=1, keepdims=True)
        prob_half = attention.astype(jnp.bfloat16)
        head_out = jnp.dot(prob_half, value_head, preferred_element_type=jnp.float32).astype(
            jnp.bfloat16
        )
        prob_grad = jnp.dot(grad_head, value_head.T, preferred_element_type=jnp.float32)
        correction = jnp.sum(attention * prob_grad, axis=1, keepdims=True)
        score_grad = (attention * (prob_grad - correction) * factor).astype(jnp.bfloat16)
        query_grad = jnp.dot(score_grad, key_head, preferred_element_type=jnp.float32).astype(
            jnp.bfloat16
        )
        key_grad = jnp.dot(score_grad.T, query_head, preferred_element_type=jnp.float32).astype(
            jnp.bfloat16
        )
        value_grad = jnp.dot(prob_half.T, grad_head, preferred_element_type=jnp.float32).astype(
            jnp.bfloat16
        )
        return (head_out, query_grad, key_grad, value_grad)

    def join_heads(stacked):
        return jnp.transpose(stacked, (1, 0, 2)).reshape(stacked.shape[1], model_width)

    stacked = lax.map(one_head, jnp.arange(HEADS, dtype=jnp.int32))
    attn_out, query_grad, key_grad, value_grad = [
        join_heads(stacked_part) for stacked_part in stacked
    ]
    part_output = jnp.dot(attn_out.T, upstream, preferred_element_type=jnp.float32)
    grad_grid = jnp.dot(query_grad, query_weight.T, preferred_element_type=jnp.float32).astype(
        jnp.bfloat16
    )
    part_query = jnp.dot(grid_rows.T, query_grad, preferred_element_type=jnp.float32)
    return (grad_grid, key_grad, value_grad, part_output, part_query)


def send_slots(outgoing):
    arrived = lax.all_to_all(
        outgoing, ("inline", "crosslin"), split_axis=0, concat_axis=0, tiled=True
    )
    return arrived


def send_back(returned):
    result_rows = lax.all_to_all(
        returned, ("inline", "crosslin"), split_axis=0, concat_axis=0, tiled=True
    )
    return result_rows


def on_device(
    grid_feat,
    cotangent,
    trace_feat,
    trace_dest,
    query_weight,
    key_weight,
    value_weight,
    output_weight,
):
    tile_count = lax.axis_size("inline") * lax.axis_size("crosslin")
    trace_rows = trace_feat.shape[0]
    model_width = trace_feat.shape[1]
    capacity = 2 * trace_rows * TOP // tile_count
    chosen, counts = slot_table(trace_dest, tile_count, capacity)
    picker = chosen.astype(jnp.bfloat16)
    key_rows = jnp.dot(trace_feat, key_weight, preferred_element_type=jnp.float32).astype(
        jnp.bfloat16
    )
    value_rows = jnp.dot(trace_feat, value_weight, preferred_element_type=jnp.float32).astype(
        jnp.bfloat16
    )
    flag = jnp.ones((trace_rows, 128), jnp.bfloat16)
    packed = jnp.concatenate([key_rows, value_rows, trace_feat, flag], axis=1)
    outgoing = jnp.einsum(
        "tjr,rd->tjd", picker, packed, preferred_element_type=jnp.float32
    ).astype(jnp.bfloat16)
    arrived = send_slots(outgoing)
    arrived = arrived.reshape(tile_count * capacity, packed.shape[1])
    key_tile = arrived[:, :model_width]
    value_tile = arrived[:, model_width : 2 * model_width]
    feat_tile = arrived[:, 2 * model_width : 3 * model_width]
    live_slots = arrived[:, 3 * model_width] > 0.5
    grad_grid, key_grad, value_grad, part_output, part_query = tile_grad(
        grid_feat, cotangent, query_weight, output_weight, key_tile, value_tile, live_slots
    )
    part_key = jnp.dot(feat_tile.T, key_grad, preferred_element_type=jnp.float32)
    part_value = jnp.dot(feat_tile.T, value_grad, preferred_element_type=jnp.float32)
    grad_query, grad_key, grad_value, grad_output = lax.psum(
        (part_query, part_key, part_value, part_output), ("inline", "crosslin")
    )
    slot_trace = jnp.dot(key_grad, key_weight.T, preferred_element_type=jnp.float32)
    slot_trace = slot_trace + jnp.dot(
        value_grad, value_weight.T, preferred_element_type=jnp.float32
    )
    slot_trace = slot_trace.astype(jnp.bfloat16).reshape(tile_count, capacity, model_width)
    returned = send_back(slot_trace)
    grad_trace = jnp.einsum("tjr,tje->re", picker, returned, preferred_element_type=jnp.float32)
    return (grad_grid, grad_trace, grad_query, grad_key, grad_value, grad_output)


def solution(mesh):
    in_specs = (
        P(("inline", "crosslin"), None),
        P(("inline", "crosslin"), None),
        P(("inline", "crosslin"), None),
        P(("inline", "crosslin"), None),
        P(),
        P(),
        P(),
        P(),
    )
    out_specs = (
        P(("inline", "crosslin"), None),
        P(("inline", "crosslin"), None),
        P(),
        P(),
        P(),
        P(),
    )
    return jax.shard_map(
        on_device, mesh=mesh, in_specs=in_specs, out_specs=out_specs, check_vma=False
    )
```

```python
import jax
import jax.numpy as jnp
from jax import lax
from jax.experimental import pallas as pl
from jax.experimental.pallas import tpu as pltpu
from jax.sharding import PartitionSpec as P

HEADS = 8
TOP = 2


def slot_table(targets, tile_count, capacity):
    tile_ids = jnp.arange(tile_count, dtype=jnp.int32)
    named = jnp.any(targets[:, :, None] == tile_ids[None, None, :], axis=1)
    position = jnp.cumsum(named.astype(jnp.int32), axis=0) - 1
    places = jnp.arange(capacity, dtype=jnp.int32)
    chosen = named.T[:, None, :] & (position.T[:, None, :] == places[None, :, None])
    return (chosen, jnp.sum(named.astype(jnp.int32), axis=0))


def attention_kernel(q_ref, g_ref, k_ref, v_ref, live_ref, o_ref, dq_ref, dk_ref, dv_ref, dk_acc, dv_acc):
    step = pl.program_id(0)
    width = q_ref.shape[1]
    head_size = width // HEADS
    factor = head_size ** (-0.5)

    @pl.when(step == 0)
    def _():
        dk_acc[...] = jnp.zeros_like(dk_acc)
        dv_acc[...] = jnp.zeros_like(dv_acc)

    live = live_ref[...] > 0.5
    for h in range(HEADS):
        cols = slice(h * head_size, (h + 1) * head_size)
        q_h = q_ref[:, cols]
        g_h = g_ref[:, cols]
        k_h = k_ref[:, cols]
        v_h = v_ref[:, cols]
        nt = (((1,), (1,)), ((), ()))
        tn = (((0,), (0,)), ((), ()))
        scores = lax.dot_general(q_h, k_h, nt, preferred_element_type=jnp.float32) * factor
        scores = jnp.where(live, scores, -1e30)
        peak = jnp.max(scores, axis=1, keepdims=True)
        raised = jnp.exp(scores - peak)
        attention = raised / jnp.sum(raised, axis=1, keepdims=True)
        prob_half = attention.astype(jnp.bfloat16)
        o_ref[:, cols] = jnp.dot(prob_half, v_h, preferred_element_type=jnp.float32).astype(o_ref.dtype)
        prob_grad = lax.dot_general(g_h, v_h, nt, preferred_element_type=jnp.float32)
        correction = jnp.sum(attention * prob_grad, axis=1, keepdims=True)
        score_grad = (attention * (prob_grad - correction) * factor).astype(jnp.bfloat16)
        dq_ref[:, cols] = jnp.dot(score_grad, k_h, preferred_element_type=jnp.float32).astype(dq_ref.dtype)
        dk_acc[:, cols] += lax.dot_general(score_grad, q_h, tn, preferred_element_type=jnp.float32)
        dv_acc[:, cols] += lax.dot_general(prob_half, g_h, tn, preferred_element_type=jnp.float32)

    @pl.when(step == pl.num_programs(0) - 1)
    def _():
        dk_ref[...] = dk_acc[...].astype(dk_ref.dtype)
        dv_ref[...] = dv_acc[...].astype(dv_ref.dtype)


def fused_attention(queries, out_grad, key_tile, value_tile, live, block=256):
    rows, width = queries.shape
    slots = key_tile.shape[0]
    row_block = pl.BlockSpec((block, width), lambda i: (i, 0))
    slot_block = pl.BlockSpec((slots, width), lambda i: (0, 0))
    live_block = pl.BlockSpec((1, slots), lambda i: (0, 0))
    return pl.pallas_call(
        attention_kernel,
        grid=(rows // block,),
        in_specs=[row_block, row_block, slot_block, slot_block, live_block],
        out_specs=[row_block, row_block, slot_block, slot_block],
        out_shape=[
            jax.ShapeDtypeStruct((rows, width), jnp.bfloat16),
            jax.ShapeDtypeStruct((rows, width), jnp.bfloat16),
            jax.ShapeDtypeStruct((slots, width), jnp.bfloat16),
            jax.ShapeDtypeStruct((slots, width), jnp.bfloat16),
        ],
        scratch_shapes=[pltpu.VMEM((slots, width), jnp.float32), pltpu.VMEM((slots, width), jnp.float32)],
        compiler_params=pltpu.CompilerParams(dimension_semantics=("arbitrary",)),
    )(queries, out_grad, key_tile, value_tile, live.astype(jnp.float32).reshape(1, slots))


def tile_grad(grid_rows, upstream, query_weight, output_weight, key_tile, value_tile, live_slots):
    queries = jnp.dot(grid_rows, query_weight, preferred_element_type=jnp.float32).astype(
        jnp.bfloat16
    )
    out_grad = jnp.dot(upstream, output_weight.T, preferred_element_type=jnp.float32).astype(
        jnp.bfloat16
    )
    attn_out, query_grad, key_grad, value_grad = fused_attention(
        queries, out_grad, key_tile, value_tile, live_slots
    )
    part_output = jnp.dot(attn_out.T, upstream, preferred_element_type=jnp.float32)
    grad_grid = jnp.dot(query_grad, query_weight.T, preferred_element_type=jnp.float32).astype(
        jnp.bfloat16
    )
    part_query = jnp.dot(grid_rows.T, query_grad, preferred_element_type=jnp.float32)
    return (grad_grid, key_grad, value_grad, part_output, part_query)


def send_slots(outgoing):
    arrived = lax.all_to_all(
        outgoing, ("inline", "crosslin"), split_axis=0, concat_axis=0, tiled=True
    )
    return arrived


def send_back(returned):
    result_rows = lax.all_to_all(
        returned, ("inline", "crosslin"), split_axis=0, concat_axis=0, tiled=True
    )
    return result_rows


def on_device(
    grid_feat,
    cotangent,
    trace_feat,
    trace_dest,
    query_weight,
    key_weight,
    value_weight,
    output_weight,
):
    tile_count = lax.axis_size("inline") * lax.axis_size("crosslin")
    trace_rows = trace_feat.shape[0]
    model_width = trace_feat.shape[1]
    capacity = 2 * trace_rows * TOP // tile_count
    chosen, counts = slot_table(trace_dest, tile_count, capacity)
    picker = chosen.astype(jnp.bfloat16)
    key_rows = jnp.dot(trace_feat, key_weight, preferred_element_type=jnp.float32).astype(
        jnp.bfloat16
    )
    value_rows = jnp.dot(trace_feat, value_weight, preferred_element_type=jnp.float32).astype(
        jnp.bfloat16
    )
    flag = jnp.ones((trace_rows, 128), jnp.bfloat16)
    packed = jnp.concatenate([key_rows, value_rows, trace_feat, flag], axis=1)
    outgoing = jnp.einsum(
        "tjr,rd->tjd", picker, packed, preferred_element_type=jnp.float32
    ).astype(jnp.bfloat16)
    arrived = send_slots(outgoing)
    arrived = arrived.reshape(tile_count * capacity, packed.shape[1])
    key_tile = arrived[:, :model_width]
    value_tile = arrived[:, model_width : 2 * model_width]
    feat_tile = arrived[:, 2 * model_width : 3 * model_width]
    live_slots = arrived[:, 3 * model_width] > 0.5
    grad_grid, key_grad, value_grad, part_output, part_query = tile_grad(
        grid_feat, cotangent, query_weight, output_weight, key_tile, value_tile, live_slots
    )
    part_key = jnp.dot(feat_tile.T, key_grad, preferred_element_type=jnp.float32)
    part_value = jnp.dot(feat_tile.T, value_grad, preferred_element_type=jnp.float32)
    grad_query, grad_key, grad_value, grad_output = lax.psum(
        (part_query, part_key, part_value, part_output), ("inline", "crosslin")
    )
    slot_trace = jnp.dot(key_grad, key_weight.T, preferred_element_type=jnp.float32)
    slot_trace = slot_trace + jnp.dot(
        value_grad, value_weight.T, preferred_element_type=jnp.float32
    )
    slot_trace = slot_trace.astype(jnp.bfloat16).reshape(tile_count, capacity, model_width)
    returned = send_back(slot_trace)
    grad_trace = jnp.einsum("tjr,tje->re", picker, returned, preferred_element_type=jnp.float32)
    return (grad_grid, grad_trace, grad_query, grad_key, grad_value, grad_output)


def solution(mesh):
    in_specs = (
        P(("inline", "crosslin"), None),
        P(("inline", "crosslin"), None),
        P(("inline", "crosslin"), None),
        P(("inline", "crosslin"), None),
        P(),
        P(),
        P(),
        P(),
    )
    out_specs = (
        P(("inline", "crosslin"), None),
        P(("inline", "crosslin"), None),
        P(),
        P(),
        P(),
        P(),
    )
    return jax.shard_map(
        on_device, mesh=mesh, in_specs=in_specs, out_specs=out_specs, check_vma=False
    )
```

```python
import jax
import jax.numpy as jnp
from jax import lax
from jax.experimental import pallas as pl
from jax.experimental.pallas import tpu as pltpu
from jax.sharding import PartitionSpec as P

HEADS = 8
TOP = 2


def slot_table(targets, tile_count, capacity):
    tile_ids = jnp.arange(tile_count, dtype=jnp.int32)
    named = jnp.any(targets[:, :, None] == tile_ids[None, None, :], axis=1)
    position = jnp.cumsum(named.astype(jnp.int32), axis=0) - 1
    places = jnp.arange(capacity, dtype=jnp.int32)
    chosen = named.T[:, None, :] & (position.T[:, None, :] == places[None, :, None])
    return (chosen, jnp.sum(named.astype(jnp.int32), axis=0))


def attention_kernel(q_ref, g_ref, k_ref, v_ref, live_ref, o_ref, dq_ref, dk_ref, dv_ref, dk_acc, dv_acc):
    step = pl.program_id(0)
    width = q_ref.shape[1]
    head_size = width // HEADS
    factor = head_size ** (-0.5)

    @pl.when(step == 0)
    def _():
        dk_acc[...] = jnp.zeros_like(dk_acc)
        dv_acc[...] = jnp.zeros_like(dv_acc)

    live = live_ref[...] > 0.5
    for h in range(HEADS):
        cols = slice(h * head_size, (h + 1) * head_size)
        q_h = q_ref[:, cols]
        g_h = g_ref[:, cols]
        k_h = k_ref[:, cols]
        v_h = v_ref[:, cols]
        nt = (((1,), (1,)), ((), ()))
        tn = (((0,), (0,)), ((), ()))
        scores = lax.dot_general(q_h, k_h, nt, preferred_element_type=jnp.float32) * factor
        scores = jnp.where(live, scores, -1e30)
        peak = jnp.max(scores, axis=1, keepdims=True)
        raised = jnp.exp(scores - peak)
        attention = raised / jnp.sum(raised, axis=1, keepdims=True)
        prob_half = attention.astype(jnp.bfloat16)
        o_ref[:, cols] = jnp.dot(prob_half, v_h, preferred_element_type=jnp.float32).astype(o_ref.dtype)
        prob_grad = lax.dot_general(g_h, v_h, nt, preferred_element_type=jnp.float32)
        correction = jnp.sum(attention * prob_grad, axis=1, keepdims=True)
        score_grad = (attention * (prob_grad - correction) * factor).astype(jnp.bfloat16)
        dq_ref[:, cols] = jnp.dot(score_grad, k_h, preferred_element_type=jnp.float32).astype(dq_ref.dtype)
        dk_acc[:, cols] += lax.dot_general(score_grad, q_h, tn, preferred_element_type=jnp.float32)
        dv_acc[:, cols] += lax.dot_general(prob_half, g_h, tn, preferred_element_type=jnp.float32)

    @pl.when(step == pl.num_programs(0) - 1)
    def _():
        dk_ref[...] = dk_acc[...].astype(dk_ref.dtype)
        dv_ref[...] = dv_acc[...].astype(dv_ref.dtype)


def fused_attention(queries, out_grad, key_tile, value_tile, live, block=512):
    rows, width = queries.shape
    slots = key_tile.shape[0]
    row_block = pl.BlockSpec((block, width), lambda i: (i, 0))
    slot_block = pl.BlockSpec((slots, width), lambda i: (0, 0))
    live_block = pl.BlockSpec((1, slots), lambda i: (0, 0))
    return pl.pallas_call(
        attention_kernel,
        grid=(rows // block,),
        in_specs=[row_block, row_block, slot_block, slot_block, live_block],
        out_specs=[row_block, row_block, slot_block, slot_block],
        out_shape=[
            jax.ShapeDtypeStruct((rows, width), jnp.bfloat16),
            jax.ShapeDtypeStruct((rows, width), jnp.bfloat16),
            jax.ShapeDtypeStruct((slots, width), jnp.bfloat16),
            jax.ShapeDtypeStruct((slots, width), jnp.bfloat16),
        ],
        scratch_shapes=[pltpu.VMEM((slots, width), jnp.float32), pltpu.VMEM((slots, width), jnp.float32)],
        compiler_params=pltpu.CompilerParams(dimension_semantics=("arbitrary",)),
    )(queries, out_grad, key_tile, value_tile, live.astype(jnp.float32).reshape(1, slots))


def tile_grad(grid_rows, upstream, query_weight, output_weight, key_tile, value_tile, live_slots):
    queries = jnp.dot(grid_rows, query_weight, preferred_element_type=jnp.float32).astype(
        jnp.bfloat16
    )
    out_grad = jnp.dot(upstream, output_weight.T, preferred_element_type=jnp.float32).astype(
        jnp.bfloat16
    )
    attn_out, query_grad, key_grad, value_grad = fused_attention(
        queries, out_grad, key_tile, value_tile, live_slots
    )
    part_output = jnp.dot(attn_out.T, upstream, preferred_element_type=jnp.float32)
    grad_grid = jnp.dot(query_grad, query_weight.T, preferred_element_type=jnp.float32).astype(
        jnp.bfloat16
    )
    part_query = jnp.dot(grid_rows.T, query_grad, preferred_element_type=jnp.float32)
    return (grad_grid, key_grad, value_grad, part_output, part_query)


def send_slots(outgoing):
    arrived = lax.all_to_all(
        outgoing, ("inline", "crosslin"), split_axis=0, concat_axis=0, tiled=True
    )
    return arrived


def send_back(returned):
    result_rows = lax.all_to_all(
        returned, ("inline", "crosslin"), split_axis=0, concat_axis=0, tiled=True
    )
    return result_rows


def on_device(
    grid_feat,
    cotangent,
    trace_feat,
    trace_dest,
    query_weight,
    key_weight,
    value_weight,
    output_weight,
):
    tile_count = lax.axis_size("inline") * lax.axis_size("crosslin")
    trace_rows = trace_feat.shape[0]
    model_width = trace_feat.shape[1]
    capacity = 2 * trace_rows * TOP // tile_count
    chosen, counts = slot_table(trace_dest, tile_count, capacity)
    picker = chosen.astype(jnp.bfloat16)
    key_rows = jnp.dot(trace_feat, key_weight, preferred_element_type=jnp.float32).astype(
        jnp.bfloat16
    )
    value_rows = jnp.dot(trace_feat, value_weight, preferred_element_type=jnp.float32).astype(
        jnp.bfloat16
    )
    flag = jnp.ones((trace_rows, 128), jnp.bfloat16)
    picker = picker.reshape(tile_count * capacity, trace_rows)
    packed = jnp.concatenate([key_rows, value_rows, flag], axis=1)
    outgoing = jnp.dot(picker, packed, preferred_element_type=jnp.float32).astype(jnp.bfloat16)
    feat_out = jnp.dot(picker, trace_feat, preferred_element_type=jnp.float32).astype(jnp.bfloat16)
    arrived = send_slots(outgoing)
    arrived, feat_out = lax.optimization_barrier((arrived, feat_out))
    feat_tile = send_slots(feat_out)
    key_tile = arrived[:, :model_width]
    value_tile = arrived[:, model_width : 2 * model_width]
    live_slots = arrived[:, 2 * model_width] > 0.5
    grad_grid, key_grad, value_grad, part_output, part_query = tile_grad(
        grid_feat, cotangent, query_weight, output_weight, key_tile, value_tile, live_slots
    )
    part_key = jnp.dot(feat_tile.T, key_grad, preferred_element_type=jnp.float32)
    part_value = jnp.dot(feat_tile.T, value_grad, preferred_element_type=jnp.float32)
    grad_query, grad_key, grad_value, grad_output = lax.psum(
        (part_query, part_key, part_value, part_output), ("inline", "crosslin")
    )
    slot_trace = jnp.dot(key_grad, key_weight.T, preferred_element_type=jnp.float32)
    slot_trace = slot_trace + jnp.dot(
        value_grad, value_weight.T, preferred_element_type=jnp.float32
    )
    returned = send_back(slot_trace.astype(jnp.bfloat16))
    grad_trace = jnp.dot(picker.T, returned, preferred_element_type=jnp.float32)
    return (grad_grid, grad_trace, grad_query, grad_key, grad_value, grad_output)


def solution(mesh):
    in_specs = (
        P(("inline", "crosslin"), None),
        P(("inline", "crosslin"), None),
        P(("inline", "crosslin"), None),
        P(("inline", "crosslin"), None),
        P(),
        P(),
        P(),
        P(),
    )
    out_specs = (
        P(("inline", "crosslin"), None),
        P(("inline", "crosslin"), None),
        P(),
        P(),
        P(),
        P(),
    )
    return jax.shard_map(
        on_device, mesh=mesh, in_specs=in_specs, out_specs=out_specs, check_vma=False
    )
```

```python
import jax
import jax.numpy as jnp
from jax import lax
from jax.experimental import pallas as pl
from jax.experimental.pallas import tpu as pltpu
from jax.sharding import PartitionSpec as P

HEADS = 8
TOP = 2


def slot_table(targets, tile_count, capacity):
    tile_ids = jnp.arange(tile_count, dtype=jnp.int32)
    named = jnp.any(targets[:, :, None] == tile_ids[None, None, :], axis=1)
    position = jnp.cumsum(named.astype(jnp.int32), axis=0) - 1
    places = jnp.arange(capacity, dtype=jnp.int32)
    chosen = named.T[:, None, :] & (position.T[:, None, :] == places[None, :, None])
    return (chosen, jnp.sum(named.astype(jnp.int32), axis=0))


def attention_kernel(q_ref, g_ref, k_ref, v_ref, live_ref, o_ref, dq_ref, dk_ref, dv_ref, dk_acc, dv_acc):
    step = pl.program_id(0)
    width = q_ref.shape[1]
    head_size = width // HEADS
    factor = head_size ** (-0.5)

    @pl.when(step == 0)
    def _():
        dk_acc[...] = jnp.zeros_like(dk_acc)
        dv_acc[...] = jnp.zeros_like(dv_acc)

    live = live_ref[...] > 0.5
    for h in range(HEADS):
        cols = slice(h * head_size, (h + 1) * head_size)
        q_h = q_ref[:, cols]
        g_h = g_ref[:, cols]
        k_h = k_ref[:, cols]
        v_h = v_ref[:, cols]
        nt = (((1,), (1,)), ((), ()))
        tn = (((0,), (0,)), ((), ()))
        scores = lax.dot_general(q_h, k_h, nt, preferred_element_type=jnp.float32) * factor
        scores = jnp.where(live, scores, -1e30)
        peak = jnp.max(scores, axis=1, keepdims=True)
        raised = jnp.exp(scores - peak)
        attention = raised / jnp.sum(raised, axis=1, keepdims=True)
        prob_half = attention.astype(jnp.bfloat16)
        o_ref[:, cols] = jnp.dot(prob_half, v_h, preferred_element_type=jnp.float32).astype(o_ref.dtype)
        prob_grad = lax.dot_general(g_h, v_h, nt, preferred_element_type=jnp.float32)
        correction = jnp.sum(attention * prob_grad, axis=1, keepdims=True)
        score_grad = (attention * (prob_grad - correction) * factor).astype(jnp.bfloat16)
        dq_ref[:, cols] = jnp.dot(score_grad, k_h, preferred_element_type=jnp.float32).astype(dq_ref.dtype)
        dk_acc[:, cols] += lax.dot_general(score_grad, q_h, tn, preferred_element_type=jnp.float32)
        dv_acc[:, cols] += lax.dot_general(prob_half, g_h, tn, preferred_element_type=jnp.float32)

    @pl.when(step == pl.num_programs(0) - 1)
    def _():
        dk_ref[...] = dk_acc[...].astype(dk_ref.dtype)
        dv_ref[...] = dv_acc[...].astype(dv_ref.dtype)


def fused_attention(queries, out_grad, key_tile, value_tile, live, block=512):
    rows, width = queries.shape
    slots = key_tile.shape[0]
    row_block = pl.BlockSpec((block, width), lambda i: (i, 0))
    slot_block = pl.BlockSpec((slots, width), lambda i: (0, 0))
    live_block = pl.BlockSpec((1, slots), lambda i: (0, 0))
    return pl.pallas_call(
        attention_kernel,
        grid=(rows // block,),
        in_specs=[row_block, row_block, slot_block, slot_block, live_block],
        out_specs=[row_block, row_block, slot_block, slot_block],
        out_shape=[
            jax.ShapeDtypeStruct((rows, width), jnp.bfloat16),
            jax.ShapeDtypeStruct((rows, width), jnp.bfloat16),
            jax.ShapeDtypeStruct((slots, width), jnp.bfloat16),
            jax.ShapeDtypeStruct((slots, width), jnp.bfloat16),
        ],
        scratch_shapes=[pltpu.VMEM((slots, width), jnp.float32), pltpu.VMEM((slots, width), jnp.float32)],
        compiler_params=pltpu.CompilerParams(dimension_semantics=("arbitrary",)),
    )(queries, out_grad, key_tile, value_tile, live.astype(jnp.float32).reshape(1, slots))


def tile_grad(grid_rows, upstream, query_weight, output_weight, key_tile, value_tile, live_slots):
    queries = jnp.dot(grid_rows, query_weight, preferred_element_type=jnp.float32).astype(
        jnp.bfloat16
    )
    out_grad = jnp.dot(upstream, output_weight.T, preferred_element_type=jnp.float32).astype(
        jnp.bfloat16
    )
    attn_out, query_grad, key_grad, value_grad = fused_attention(
        queries, out_grad, key_tile, value_tile, live_slots
    )
    part_output = jnp.dot(attn_out.T, upstream, preferred_element_type=jnp.float32)
    grad_grid = jnp.dot(query_grad, query_weight.T, preferred_element_type=jnp.float32).astype(
        jnp.bfloat16
    )
    part_query = jnp.dot(grid_rows.T, query_grad, preferred_element_type=jnp.float32)
    return (grad_grid, key_grad, value_grad, part_output, part_query)


def send_slots(outgoing):
    arrived = lax.all_to_all(
        outgoing, ("inline", "crosslin"), split_axis=0, concat_axis=0, tiled=True
    )
    return arrived


def send_back(returned):
    result_rows = lax.all_to_all(
        returned, ("inline", "crosslin"), split_axis=0, concat_axis=0, tiled=True
    )
    return result_rows


def sum_over_devices(parts):
    count = lax.axis_size("inline") * lax.axis_size("crosslin")
    stacked = jnp.stack(parts)
    pieces = stacked.reshape(count, stacked.size // (count * stacked.shape[-1]), stacked.shape[-1])
    mine = send_slots(pieces).sum(axis=0, keepdims=True)
    gathered = send_slots(jnp.broadcast_to(mine, pieces.shape)).reshape(stacked.shape)
    return tuple(gathered[i] for i in range(len(parts)))


def on_device(
    grid_feat,
    cotangent,
    trace_feat,
    trace_dest,
    query_weight,
    key_weight,
    value_weight,
    output_weight,
):
    tile_count = lax.axis_size("inline") * lax.axis_size("crosslin")
    trace_rows = trace_feat.shape[0]
    model_width = trace_feat.shape[1]
    capacity = 2 * trace_rows * TOP // tile_count
    chosen, counts = slot_table(trace_dest, tile_count, capacity)
    picker = chosen.astype(jnp.bfloat16)
    key_rows = jnp.dot(trace_feat, key_weight, preferred_element_type=jnp.float32).astype(
        jnp.bfloat16
    )
    value_rows = jnp.dot(trace_feat, value_weight, preferred_element_type=jnp.float32).astype(
        jnp.bfloat16
    )
    flag = jnp.ones((trace_rows, 128), jnp.bfloat16)
    picker = picker.reshape(tile_count * capacity, trace_rows)
    packed = jnp.concatenate([key_rows, value_rows, flag], axis=1)
    outgoing = jnp.dot(picker, packed, preferred_element_type=jnp.float32).astype(jnp.bfloat16)
    feat_out = jnp.dot(picker, trace_feat, preferred_element_type=jnp.float32).astype(jnp.bfloat16)
    arrived = send_slots(outgoing)
    arrived, feat_out = lax.optimization_barrier((arrived, feat_out))
    feat_tile = send_slots(feat_out)
    key_tile = arrived[:, :model_width]
    value_tile = arrived[:, model_width : 2 * model_width]
    live_slots = arrived[:, 2 * model_width] > 0.5
    grad_grid, key_grad, value_grad, part_output, part_query = tile_grad(
        grid_feat, cotangent, query_weight, output_weight, key_tile, value_tile, live_slots
    )
    part_key = jnp.dot(feat_tile.T, key_grad, preferred_element_type=jnp.float32)
    part_value = jnp.dot(feat_tile.T, value_grad, preferred_element_type=jnp.float32)
    grad_query, grad_key, grad_value, grad_output = sum_over_devices(
        (part_query, part_key, part_value, part_output)
    )
    slot_trace = jnp.dot(key_grad, key_weight.T, preferred_element_type=jnp.float32)
    slot_trace = slot_trace + jnp.dot(
        value_grad, value_weight.T, preferred_element_type=jnp.float32
    )
    returned = send_back(slot_trace.astype(jnp.bfloat16))
    grad_trace = jnp.dot(picker.T, returned, preferred_element_type=jnp.float32)
    return (grad_grid, grad_trace, grad_query, grad_key, grad_value, grad_output)


def solution(mesh):
    in_specs = (
        P(("inline", "crosslin"), None),
        P(("inline", "crosslin"), None),
        P(("inline", "crosslin"), None),
        P(("inline", "crosslin"), None),
        P(),
        P(),
        P(),
        P(),
    )
    out_specs = (
        P(("inline", "crosslin"), None),
        P(("inline", "crosslin"), None),
        P(),
        P(),
        P(),
        P(),
    )
    return jax.shard_map(
        on_device, mesh=mesh, in_specs=in_specs, out_specs=out_specs, check_vma=False
    )
```

```python
import jax
import jax.numpy as jnp
from jax import lax
from jax.experimental import pallas as pl
from jax.experimental.pallas import tpu as pltpu
from jax.sharding import PartitionSpec as P

HEADS = 8
TOP = 2


def slot_table(targets, tile_count, capacity):
    tile_ids = jnp.arange(tile_count, dtype=jnp.int32)
    named = jnp.any(targets[:, :, None] == tile_ids[None, None, :], axis=1)
    position = jnp.cumsum(named.astype(jnp.int32), axis=0) - 1
    places = jnp.arange(capacity, dtype=jnp.int32)
    chosen = named.T[:, None, :] & (position.T[:, None, :] == places[None, :, None])
    return (chosen, jnp.sum(named.astype(jnp.int32), axis=0))


def attention_kernel(q_ref, g_ref, k_ref, v_ref, live_ref, o_ref, dq_ref, dk_ref, dv_ref, dk_acc, dv_acc):
    step = pl.program_id(0)
    width = q_ref.shape[1]
    head_size = width // HEADS
    factor = head_size ** (-0.5)

    @pl.when(step == 0)
    def _():
        dk_acc[...] = jnp.zeros_like(dk_acc)
        dv_acc[...] = jnp.zeros_like(dv_acc)

    live = live_ref[...] > 0.5
    for h in range(HEADS):
        cols = slice(h * head_size, (h + 1) * head_size)
        q_h = q_ref[:, cols]
        g_h = g_ref[:, cols]
        k_h = k_ref[:, cols]
        v_h = v_ref[:, cols]
        nt = (((1,), (1,)), ((), ()))
        tn = (((0,), (0,)), ((), ()))
        scores = lax.dot_general(q_h, k_h, nt, preferred_element_type=jnp.float32) * factor
        scores = jnp.where(live, scores, -1e30)
        peak = jnp.max(scores, axis=1, keepdims=True)
        raised = jnp.exp(scores - peak)
        attention = raised / jnp.sum(raised, axis=1, keepdims=True)
        prob_half = attention.astype(jnp.bfloat16)
        o_ref[:, cols] = jnp.dot(prob_half, v_h, preferred_element_type=jnp.float32).astype(o_ref.dtype)
        prob_grad = lax.dot_general(g_h, v_h, nt, preferred_element_type=jnp.float32)
        correction = jnp.sum(attention * prob_grad, axis=1, keepdims=True)
        score_grad = (attention * (prob_grad - correction) * factor).astype(jnp.bfloat16)
        dq_ref[:, cols] = jnp.dot(score_grad, k_h, preferred_element_type=jnp.float32).astype(dq_ref.dtype)
        dk_acc[:, cols] += lax.dot_general(score_grad, q_h, tn, preferred_element_type=jnp.float32)
        dv_acc[:, cols] += lax.dot_general(prob_half, g_h, tn, preferred_element_type=jnp.float32)

    @pl.when(step == pl.num_programs(0) - 1)
    def _():
        dk_ref[...] = dk_acc[...].astype(dk_ref.dtype)
        dv_ref[...] = dv_acc[...].astype(dv_ref.dtype)


def fused_attention(queries, out_grad, key_tile, value_tile, live, block=512):
    rows, width = queries.shape
    slots = key_tile.shape[0]
    row_block = pl.BlockSpec((block, width), lambda i: (i, 0))
    slot_block = pl.BlockSpec((slots, width), lambda i: (0, 0))
    live_block = pl.BlockSpec((1, slots), lambda i: (0, 0))
    return pl.pallas_call(
        attention_kernel,
        grid=(rows // block,),
        in_specs=[row_block, row_block, slot_block, slot_block, live_block],
        out_specs=[row_block, row_block, slot_block, slot_block],
        out_shape=[
            jax.ShapeDtypeStruct((rows, width), jnp.bfloat16),
            jax.ShapeDtypeStruct((rows, width), jnp.bfloat16),
            jax.ShapeDtypeStruct((slots, width), jnp.bfloat16),
            jax.ShapeDtypeStruct((slots, width), jnp.bfloat16),
        ],
        scratch_shapes=[pltpu.VMEM((slots, width), jnp.float32), pltpu.VMEM((slots, width), jnp.float32)],
        compiler_params=pltpu.CompilerParams(dimension_semantics=("arbitrary",)),
    )(queries, out_grad, key_tile, value_tile, live.astype(jnp.float32).reshape(1, slots))


def send_slots(outgoing):
    arrived = lax.all_to_all(
        outgoing, ("inline", "crosslin"), split_axis=0, concat_axis=0, tiled=True
    )
    return arrived


def send_back(returned):
    result_rows = lax.all_to_all(
        returned, ("inline", "crosslin"), split_axis=0, concat_axis=0, tiled=True
    )
    return result_rows


def sum_over_devices(parts):
    count = lax.axis_size("inline") * lax.axis_size("crosslin")
    stacked = jnp.stack(parts)
    pieces = stacked.reshape(count, stacked.size // (count * stacked.shape[-1]), stacked.shape[-1])
    mine = send_slots(pieces).sum(axis=0, keepdims=True)
    gathered = send_slots(jnp.broadcast_to(mine, pieces.shape)).reshape(stacked.shape)
    return tuple(gathered[i] for i in range(len(parts)))


def on_device(
    grid_feat,
    cotangent,
    trace_feat,
    trace_dest,
    query_weight,
    key_weight,
    value_weight,
    output_weight,
):
    tile_count = lax.axis_size("inline") * lax.axis_size("crosslin")
    trace_rows = trace_feat.shape[0]
    model_width = trace_feat.shape[1]
    capacity = 2 * trace_rows * TOP // tile_count
    chosen, counts = slot_table(trace_dest, tile_count, capacity)
    picker = chosen.astype(jnp.bfloat16).reshape(tile_count * capacity, trace_rows)
    flag = jnp.ones((trace_rows, 128), jnp.bfloat16)
    packed = jnp.concatenate([trace_feat, flag], axis=1)
    outgoing = jnp.dot(picker, packed, preferred_element_type=jnp.float32).astype(jnp.bfloat16)
    arrived = send_slots(outgoing)
    feat_tile = arrived[:, :model_width]
    live_slots = arrived[:, model_width] > 0.5
    key_tile = jnp.dot(feat_tile, key_weight, preferred_element_type=jnp.float32).astype(
        jnp.bfloat16
    )
    value_tile = jnp.dot(feat_tile, value_weight, preferred_element_type=jnp.float32).astype(
        jnp.bfloat16
    )
    queries = jnp.dot(grid_feat, query_weight, preferred_element_type=jnp.float32).astype(
        jnp.bfloat16
    )
    out_grad = jnp.dot(cotangent, output_weight.T, preferred_element_type=jnp.float32).astype(
        jnp.bfloat16
    )
    attn_out, query_grad, key_grad, value_grad = fused_attention(
        queries, out_grad, key_tile, value_tile, live_slots
    )
    slot_trace = jnp.dot(key_grad, key_weight.T, preferred_element_type=jnp.float32)
    slot_trace = slot_trace + jnp.dot(
        value_grad, value_weight.T, preferred_element_type=jnp.float32
    )
    returned = send_back(slot_trace.astype(jnp.bfloat16))
    part_output = jnp.dot(attn_out.T, cotangent, preferred_element_type=jnp.float32)
    part_query = jnp.dot(grid_feat.T, query_grad, preferred_element_type=jnp.float32)
    part_key = jnp.dot(feat_tile.T, key_grad, preferred_element_type=jnp.float32)
    part_value = jnp.dot(feat_tile.T, value_grad, preferred_element_type=jnp.float32)
    returned, parts = lax.optimization_barrier(
        (returned, (part_query, part_key, part_value, part_output))
    )
    grad_query, grad_key, grad_value, grad_output = sum_over_devices(parts)
    grad_grid = jnp.dot(query_grad, query_weight.T, preferred_element_type=jnp.float32).astype(
        jnp.bfloat16
    )
    grad_trace = jnp.dot(picker.T, returned, preferred_element_type=jnp.float32)
    return (grad_grid, grad_trace, grad_query, grad_key, grad_value, grad_output)


def solution(mesh):
    in_specs = (
        P(("inline", "crosslin"), None),
        P(("inline", "crosslin"), None),
        P(("inline", "crosslin"), None),
        P(("inline", "crosslin"), None),
        P(),
        P(),
        P(),
        P(),
    )
    out_specs = (
        P(("inline", "crosslin"), None),
        P(("inline", "crosslin"), None),
        P(),
        P(),
        P(),
        P(),
    )
    return jax.shard_map(
        on_device, mesh=mesh, in_specs=in_specs, out_specs=out_specs, check_vma=False
    )
```

```python
import jax
import jax.numpy as jnp
from jax import lax
from jax.experimental import pallas as pl
from jax.experimental.pallas import tpu as pltpu
from jax.sharding import PartitionSpec as P

HEADS = 8
TOP = 2


def slot_table(targets, tile_count, capacity):
    tile_ids = jnp.arange(tile_count, dtype=jnp.int32)
    named = jnp.any(targets[:, :, None] == tile_ids[None, None, :], axis=1)
    position = jnp.cumsum(named.astype(jnp.int32), axis=0) - 1
    places = jnp.arange(capacity, dtype=jnp.int32)
    chosen = named.T[:, None, :] & (position.T[:, None, :] == places[None, :, None])
    return (chosen, jnp.sum(named.astype(jnp.int32), axis=0))


def attention_kernel(q_ref, g_ref, k_ref, v_ref, live_ref, o_ref, dq_ref, dk_ref, dv_ref, dk_acc, dv_acc):
    step = pl.program_id(0)
    width = q_ref.shape[1]
    head_size = width // HEADS
    factor = head_size ** (-0.5)

    @pl.when(step == 0)
    def _():
        dk_acc[...] = jnp.zeros_like(dk_acc)
        dv_acc[...] = jnp.zeros_like(dv_acc)

    live = live_ref[...] > 0.5
    for h in range(HEADS):
        cols = slice(h * head_size, (h + 1) * head_size)
        q_h = q_ref[:, cols]
        g_h = g_ref[:, cols]
        k_h = k_ref[:, cols]
        v_h = v_ref[:, cols]
        nt = (((1,), (1,)), ((), ()))
        tn = (((0,), (0,)), ((), ()))
        scores = lax.dot_general(q_h, k_h, nt, preferred_element_type=jnp.float32) * factor
        scores = jnp.where(live, scores, -1e30)
        peak = jnp.max(scores, axis=1, keepdims=True)
        raised = jnp.exp(scores - peak)
        attention = raised / jnp.sum(raised, axis=1, keepdims=True)
        prob_half = attention.astype(jnp.bfloat16)
        o_ref[:, cols] = jnp.dot(prob_half, v_h, preferred_element_type=jnp.float32).astype(o_ref.dtype)
        prob_grad = lax.dot_general(g_h, v_h, nt, preferred_element_type=jnp.float32)
        correction = jnp.sum(attention * prob_grad, axis=1, keepdims=True)
        score_grad = (attention * (prob_grad - correction) * factor).astype(jnp.bfloat16)
        dq_ref[:, cols] = jnp.dot(score_grad, k_h, preferred_element_type=jnp.float32).astype(dq_ref.dtype)
        dk_acc[:, cols] += lax.dot_general(score_grad, q_h, tn, preferred_element_type=jnp.float32)
        dv_acc[:, cols] += lax.dot_general(prob_half, g_h, tn, preferred_element_type=jnp.float32)

    @pl.when(step == pl.num_programs(0) - 1)
    def _():
        dk_ref[...] = dk_acc[...].astype(dk_ref.dtype)
        dv_ref[...] = dv_acc[...].astype(dv_ref.dtype)


def fused_attention(queries, out_grad, key_tile, value_tile, live, block=512):
    rows, width = queries.shape
    slots = key_tile.shape[0]
    row_block = pl.BlockSpec((block, width), lambda i: (i, 0))
    slot_block = pl.BlockSpec((slots, width), lambda i: (0, 0))
    live_block = pl.BlockSpec((1, slots), lambda i: (0, 0))
    return pl.pallas_call(
        attention_kernel,
        grid=(rows // block,),
        in_specs=[row_block, row_block, slot_block, slot_block, live_block],
        out_specs=[row_block, row_block, slot_block, slot_block],
        out_shape=[
            jax.ShapeDtypeStruct((rows, width), jnp.bfloat16),
            jax.ShapeDtypeStruct((rows, width), jnp.bfloat16),
            jax.ShapeDtypeStruct((slots, width), jnp.bfloat16),
            jax.ShapeDtypeStruct((slots, width), jnp.bfloat16),
        ],
        scratch_shapes=[pltpu.VMEM((slots, width), jnp.float32), pltpu.VMEM((slots, width), jnp.float32)],
        compiler_params=pltpu.CompilerParams(dimension_semantics=("arbitrary",)),
    )(queries, out_grad, key_tile, value_tile, live.astype(jnp.float32).reshape(1, slots))


def send_slots(outgoing):
    arrived = lax.all_to_all(
        outgoing, ("inline", "crosslin"), split_axis=0, concat_axis=0, tiled=True
    )
    return arrived


def send_back(returned):
    result_rows = lax.all_to_all(
        returned, ("inline", "crosslin"), split_axis=0, concat_axis=0, tiled=True
    )
    return result_rows


def as_tiles(part):
    rows, cols = part.shape
    return part.reshape(rows // 8, 8, cols // 128, 128).transpose(0, 2, 1, 3)


def from_tiles(tiles, shape):
    return tiles.reshape(shape[0] // 8, shape[1] // 128, 8, 128).transpose(0, 2, 1, 3).reshape(shape)


def sum_over_devices(parts):
    count = lax.axis_size("inline") * lax.axis_size("crosslin")
    tiled = [as_tiles(part).reshape(count, -1, 128) for part in parts]
    depth = tiled[0].shape[1]
    pieces = jnp.concatenate(tiled, axis=1)
    mine = send_slots(pieces).sum(axis=0, keepdims=True)
    gathered = send_slots(jnp.broadcast_to(mine, pieces.shape))
    return tuple(
        from_tiles(gathered[:, i * depth : (i + 1) * depth], part.shape)
        for i, part in enumerate(parts)
    )


def on_device(
    grid_feat,
    cotangent,
    trace_feat,
    trace_dest,
    query_weight,
    key_weight,
    value_weight,
    output_weight,
):
    tile_count = lax.axis_size("inline") * lax.axis_size("crosslin")
    trace_rows = trace_feat.shape[0]
    model_width = trace_feat.shape[1]
    capacity = 2 * trace_rows * TOP // tile_count
    chosen, counts = slot_table(trace_dest, tile_count, capacity)
    picker = chosen.astype(jnp.bfloat16).reshape(tile_count * capacity, trace_rows)
    flag = jnp.ones((trace_rows, 128), jnp.bfloat16)
    packed = jnp.concatenate([trace_feat, flag], axis=1)
    outgoing = jnp.dot(picker, packed, preferred_element_type=jnp.float32).astype(jnp.bfloat16)
    arrived = send_slots(outgoing)
    feat_tile = arrived[:, :model_width]
    live_slots = arrived[:, model_width] > 0.5
    key_tile = jnp.dot(feat_tile, key_weight, preferred_element_type=jnp.float32).astype(
        jnp.bfloat16
    )
    value_tile = jnp.dot(feat_tile, value_weight, preferred_element_type=jnp.float32).astype(
        jnp.bfloat16
    )
    queries = jnp.dot(grid_feat, query_weight, preferred_element_type=jnp.float32).astype(
        jnp.bfloat16
    )
    out_grad = jnp.dot(cotangent, output_weight.T, preferred_element_type=jnp.float32).astype(
        jnp.bfloat16
    )
    attn_out, query_grad, key_grad, value_grad = fused_attention(
        queries, out_grad, key_tile, value_tile, live_slots
    )
    slot_trace = jnp.dot(key_grad, key_weight.T, preferred_element_type=jnp.float32)
    slot_trace = slot_trace + jnp.dot(
        value_grad, value_weight.T, preferred_element_type=jnp.float32
    )
    returned = send_back(slot_trace.astype(jnp.bfloat16))
    part_output = jnp.dot(attn_out.T, cotangent, preferred_element_type=jnp.float32)
    part_query = jnp.dot(grid_feat.T, query_grad, preferred_element_type=jnp.float32)
    part_key = jnp.dot(feat_tile.T, key_grad, preferred_element_type=jnp.float32)
    part_value = jnp.dot(feat_tile.T, value_grad, preferred_element_type=jnp.float32)
    returned, parts = lax.optimization_barrier(
        (returned, (part_query, part_key, part_value, part_output))
    )
    grad_query, grad_key, grad_value, grad_output = sum_over_devices(parts)
    grad_grid = jnp.dot(query_grad, query_weight.T, preferred_element_type=jnp.float32).astype(
        jnp.bfloat16
    )
    grad_trace = jnp.dot(picker.T, returned, preferred_element_type=jnp.float32)
    return (grad_grid, grad_trace, grad_query, grad_key, grad_value, grad_output)


def solution(mesh):
    in_specs = (
        P(("inline", "crosslin"), None),
        P(("inline", "crosslin"), None),
        P(("inline", "crosslin"), None),
        P(("inline", "crosslin"), None),
        P(),
        P(),
        P(),
        P(),
    )
    out_specs = (
        P(("inline", "crosslin"), None),
        P(("inline", "crosslin"), None),
        P(),
        P(),
        P(),
        P(),
    )
    return jax.shard_map(
        on_device, mesh=mesh, in_specs=in_specs, out_specs=out_specs, check_vma=False
    )
```

```python
import jax
import jax.numpy as jnp
from jax import lax
from jax.experimental import pallas as pl
from jax.experimental.pallas import tpu as pltpu
from jax.sharding import PartitionSpec as P

HEADS = 8
TOP = 2


def slot_table(targets, tile_count, capacity):
    tile_ids = jnp.arange(tile_count, dtype=jnp.int32)
    named = jnp.any(targets[:, :, None] == tile_ids[None, None, :], axis=1)
    position = jnp.cumsum(named.astype(jnp.int32), axis=0) - 1
    places = jnp.arange(capacity, dtype=jnp.int32)
    chosen = named.T[:, None, :] & (position.T[:, None, :] == places[None, :, None])
    return (chosen, jnp.sum(named.astype(jnp.int32), axis=0))


def attention_kernel(q_ref, g_ref, k_ref, v_ref, live_ref, o_ref, dq_ref, dk_ref, dv_ref, dk_acc, dv_acc):
    step = pl.program_id(0)
    width = q_ref.shape[1]
    head_size = width // HEADS
    factor = head_size ** (-0.5)

    @pl.when(step == 0)
    def _():
        dk_acc[...] = jnp.zeros_like(dk_acc)
        dv_acc[...] = jnp.zeros_like(dv_acc)

    live = live_ref[...] > 0.5
    for h in range(HEADS):
        cols = slice(h * head_size, (h + 1) * head_size)
        q_h = q_ref[:, cols]
        g_h = g_ref[:, cols]
        k_h = k_ref[:, cols]
        v_h = v_ref[:, cols]
        nt = (((1,), (1,)), ((), ()))
        tn = (((0,), (0,)), ((), ()))
        scores = lax.dot_general(q_h, k_h, nt, preferred_element_type=jnp.float32) * factor
        scores = jnp.where(live, scores, -1e30)
        peak = jnp.max(scores, axis=1, keepdims=True)
        raised = jnp.exp(scores - peak)
        attention = raised / jnp.sum(raised, axis=1, keepdims=True)
        prob_half = attention.astype(jnp.bfloat16)
        o_ref[:, cols] = jnp.dot(prob_half, v_h, preferred_element_type=jnp.float32).astype(o_ref.dtype)
        prob_grad = lax.dot_general(g_h, v_h, nt, preferred_element_type=jnp.float32)
        correction = jnp.sum(attention * prob_grad, axis=1, keepdims=True)
        score_grad = (attention * (prob_grad - correction) * factor).astype(jnp.bfloat16)
        dq_ref[:, cols] = jnp.dot(score_grad, k_h, preferred_element_type=jnp.float32).astype(dq_ref.dtype)
        dk_acc[:, cols] += lax.dot_general(score_grad, q_h, tn, preferred_element_type=jnp.float32)
        dv_acc[:, cols] += lax.dot_general(prob_half, g_h, tn, preferred_element_type=jnp.float32)

    @pl.when(step == pl.num_programs(0) - 1)
    def _():
        dk_ref[...] = dk_acc[...].astype(dk_ref.dtype)
        dv_ref[...] = dv_acc[...].astype(dv_ref.dtype)


def fused_attention(queries, out_grad, key_tile, value_tile, live, block=512):
    rows, width = queries.shape
    slots = key_tile.shape[0]
    row_block = pl.BlockSpec((block, width), lambda i: (i, 0))
    slot_block = pl.BlockSpec((slots, width), lambda i: (0, 0))
    live_block = pl.BlockSpec((1, slots), lambda i: (0, 0))
    return pl.pallas_call(
        attention_kernel,
        grid=(rows // block,),
        in_specs=[row_block, row_block, slot_block, slot_block, live_block],
        out_specs=[row_block, row_block, slot_block, slot_block],
        out_shape=[
            jax.ShapeDtypeStruct((rows, width), jnp.bfloat16),
            jax.ShapeDtypeStruct((rows, width), jnp.bfloat16),
            jax.ShapeDtypeStruct((slots, width), jnp.bfloat16),
            jax.ShapeDtypeStruct((slots, width), jnp.bfloat16),
        ],
        scratch_shapes=[pltpu.VMEM((slots, width), jnp.float32), pltpu.VMEM((slots, width), jnp.float32)],
        compiler_params=pltpu.CompilerParams(dimension_semantics=("arbitrary",)),
    )(queries, out_grad, key_tile, value_tile, live.astype(jnp.float32).reshape(1, slots))


def send_slots(outgoing):
    arrived = lax.all_to_all(
        outgoing, ("inline", "crosslin"), split_axis=0, concat_axis=0, tiled=True
    )
    return arrived


def send_back(returned):
    result_rows = lax.all_to_all(
        returned, ("inline", "crosslin"), split_axis=0, concat_axis=0, tiled=True
    )
    return result_rows


def as_tiles(part):
    rows, cols = part.shape
    return part.reshape(rows // 8, 8, cols // 128, 128).transpose(0, 2, 1, 3)


def from_tiles(tiles, shape):
    return tiles.reshape(shape[0] // 8, shape[1] // 128, 8, 128).transpose(0, 2, 1, 3).reshape(shape)


def sum_over_devices(parts):
    count = lax.axis_size("inline") * lax.axis_size("crosslin")
    tiled = [as_tiles(part).reshape(count, -1, 128) for part in parts]
    depth = tiled[0].shape[1]
    pieces = jnp.concatenate(tiled, axis=1)
    mine = send_slots(pieces).sum(axis=0, keepdims=True).astype(jnp.bfloat16)
    gathered = send_slots(jnp.broadcast_to(mine, pieces.shape)).astype(jnp.float32)
    return tuple(
        from_tiles(gathered[:, i * depth : (i + 1) * depth], part.shape)
        for i, part in enumerate(parts)
    )


def on_device(
    grid_feat,
    cotangent,
    trace_feat,
    trace_dest,
    query_weight,
    key_weight,
    value_weight,
    output_weight,
):
    tile_count = lax.axis_size("inline") * lax.axis_size("crosslin")
    trace_rows = trace_feat.shape[0]
    model_width = trace_feat.shape[1]
    capacity = 2 * trace_rows * TOP // tile_count
    chosen, counts = slot_table(trace_dest, tile_count, capacity)
    picker = chosen.astype(jnp.bfloat16).reshape(tile_count * capacity, trace_rows)
    flag = jnp.ones((trace_rows, 128), jnp.bfloat16)
    packed = jnp.concatenate([trace_feat, flag], axis=1)
    outgoing = jnp.dot(picker, packed, preferred_element_type=jnp.float32).astype(jnp.bfloat16)
    arrived = send_slots(outgoing)
    feat_tile = arrived[:, :model_width]
    live_slots = arrived[:, model_width] > 0.5
    key_tile = jnp.dot(feat_tile, key_weight, preferred_element_type=jnp.float32).astype(
        jnp.bfloat16
    )
    value_tile = jnp.dot(feat_tile, value_weight, preferred_element_type=jnp.float32).astype(
        jnp.bfloat16
    )
    queries = jnp.dot(grid_feat, query_weight, preferred_element_type=jnp.float32).astype(
        jnp.bfloat16
    )
    out_grad = jnp.dot(cotangent, output_weight.T, preferred_element_type=jnp.float32).astype(
        jnp.bfloat16
    )
    attn_out, query_grad, key_grad, value_grad = fused_attention(
        queries, out_grad, key_tile, value_tile, live_slots
    )
    slot_trace = jnp.dot(key_grad, key_weight.T, preferred_element_type=jnp.float32)
    slot_trace = slot_trace + jnp.dot(
        value_grad, value_weight.T, preferred_element_type=jnp.float32
    )
    returned = send_back(slot_trace.astype(jnp.bfloat16))
    part_output = jnp.dot(attn_out.T, cotangent, preferred_element_type=jnp.float32)
    part_query = jnp.dot(grid_feat.T, query_grad, preferred_element_type=jnp.float32)
    part_key = jnp.dot(feat_tile.T, key_grad, preferred_element_type=jnp.float32)
    part_value = jnp.dot(feat_tile.T, value_grad, preferred_element_type=jnp.float32)
    returned, parts = lax.optimization_barrier(
        (returned, (part_query, part_key, part_value, part_output))
    )
    grad_query, grad_key, grad_value, grad_output = sum_over_devices(parts)
    grad_grid = jnp.dot(query_grad, query_weight.T, preferred_element_type=jnp.float32).astype(
        jnp.bfloat16
    )
    grad_trace = jnp.dot(picker.T, returned, preferred_element_type=jnp.float32)
    return (grad_grid, grad_trace, grad_query, grad_key, grad_value, grad_output)


def solution(mesh):
    in_specs = (
        P(("inline", "crosslin"), None),
        P(("inline", "crosslin"), None),
        P(("inline", "crosslin"), None),
        P(("inline", "crosslin"), None),
        P(),
        P(),
        P(),
        P(),
    )
    out_specs = (
        P(("inline", "crosslin"), None),
        P(("inline", "crosslin"), None),
        P(),
        P(),
        P(),
        P(),
    )
    return jax.shard_map(
        on_device, mesh=mesh, in_specs=in_specs, out_specs=out_specs, check_vma=False
    )
```

```python
import jax
import jax.numpy as jnp
from jax import lax
from jax.experimental import pallas as pl
from jax.experimental.pallas import tpu as pltpu
from jax.sharding import PartitionSpec as P

HEADS = 8
TOP = 2


def slot_table(targets, tile_count, capacity):
    tile_ids = jnp.arange(tile_count, dtype=jnp.int32)
    named = jnp.any(targets[:, :, None] == tile_ids[None, None, :], axis=1)
    position = jnp.cumsum(named.astype(jnp.int32), axis=0) - 1
    places = jnp.arange(capacity, dtype=jnp.int32)
    chosen = named.T[:, None, :] & (position.T[:, None, :] == places[None, :, None])
    return (chosen, jnp.sum(named.astype(jnp.int32), axis=0))


def attention_kernel(q_ref, g_ref, k_ref, v_ref, live_ref, o_ref, dq_ref, dk_ref, dv_ref, dk_acc, dv_acc):
    step = pl.program_id(0)
    width = q_ref.shape[1]
    head_size = width // HEADS
    factor = head_size ** (-0.5)

    @pl.when(step == 0)
    def _():
        dk_acc[...] = jnp.zeros_like(dk_acc)
        dv_acc[...] = jnp.zeros_like(dv_acc)

    live = live_ref[...] > 0.5
    for h in range(HEADS):
        cols = slice(h * head_size, (h + 1) * head_size)
        q_h = q_ref[:, cols]
        g_h = g_ref[:, cols]
        k_h = k_ref[:, cols]
        v_h = v_ref[:, cols]
        nt = (((1,), (1,)), ((), ()))
        tn = (((0,), (0,)), ((), ()))
        scores = lax.dot_general(q_h, k_h, nt, preferred_element_type=jnp.float32) * factor
        scores = jnp.where(live, scores, -1e30)
        peak = jnp.max(scores, axis=1, keepdims=True)
        raised = jnp.exp(scores - peak)
        attention = raised / jnp.sum(raised, axis=1, keepdims=True)
        prob_half = attention.astype(jnp.bfloat16)
        o_ref[:, cols] = jnp.dot(prob_half, v_h, preferred_element_type=jnp.float32).astype(o_ref.dtype)
        prob_grad = lax.dot_general(g_h, v_h, nt, preferred_element_type=jnp.float32)
        correction = jnp.sum(attention * prob_grad, axis=1, keepdims=True)
        score_grad = (attention * (prob_grad - correction) * factor).astype(jnp.bfloat16)
        dq_ref[:, cols] = jnp.dot(score_grad, k_h, preferred_element_type=jnp.float32).astype(dq_ref.dtype)
        dk_acc[:, cols] += lax.dot_general(score_grad, q_h, tn, preferred_element_type=jnp.float32)
        dv_acc[:, cols] += lax.dot_general(prob_half, g_h, tn, preferred_element_type=jnp.float32)

    @pl.when(step == pl.num_programs(0) - 1)
    def _():
        dk_ref[...] = dk_acc[...].astype(dk_ref.dtype)
        dv_ref[...] = dv_acc[...].astype(dv_ref.dtype)


def fused_attention(queries, out_grad, key_tile, value_tile, live, block=512):
    rows, width = queries.shape
    slots = key_tile.shape[0]
    row_block = pl.BlockSpec((block, width), lambda i: (i, 0))
    slot_block = pl.BlockSpec((slots, width), lambda i: (0, 0))
    live_block = pl.BlockSpec((1, slots), lambda i: (0, 0))
    return pl.pallas_call(
        attention_kernel,
        grid=(rows // block,),
        in_specs=[row_block, row_block, slot_block, slot_block, live_block],
        out_specs=[row_block, row_block, slot_block, slot_block],
        out_shape=[
            jax.ShapeDtypeStruct((rows, width), jnp.bfloat16),
            jax.ShapeDtypeStruct((rows, width), jnp.bfloat16),
            jax.ShapeDtypeStruct((slots, width), jnp.bfloat16),
            jax.ShapeDtypeStruct((slots, width), jnp.bfloat16),
        ],
        scratch_shapes=[pltpu.VMEM((slots, width), jnp.float32), pltpu.VMEM((slots, width), jnp.float32)],
        compiler_params=pltpu.CompilerParams(dimension_semantics=("arbitrary",)),
    )(queries, out_grad, key_tile, value_tile, live.astype(jnp.float32).reshape(1, slots))


def send_slots(outgoing):
    arrived = lax.all_to_all(
        outgoing, ("inline", "crosslin"), split_axis=0, concat_axis=0, tiled=True
    )
    return arrived


def as_tiles(part):
    rows, cols = part.shape
    return part.reshape(rows // 8, 8, cols // 128, 128).transpose(0, 2, 1, 3)


def from_tiles(tiles, shape):
    return tiles.reshape(shape[0] // 8, shape[1] // 128, 8, 128).transpose(0, 2, 1, 3).reshape(shape)


def sum_over_devices(parts, rider):
    count = lax.axis_size("inline") * lax.axis_size("crosslin")
    tiled = [as_tiles(part).reshape(count, -1, 128) for part in parts]
    depth = tiled[0].shape[1]
    pieces = jnp.concatenate(tiled, axis=1)
    mine = send_slots(pieces).sum(axis=0, keepdims=True).astype(jnp.bfloat16)
    rider_rows = rider.size // (count * 128)
    payload = jnp.concatenate(
        [jnp.broadcast_to(mine, pieces.shape), rider.reshape(count, rider_rows, 128)], axis=1
    )
    arrived = send_slots(payload)
    gathered = arrived[:, : pieces.shape[1]].astype(jnp.float32)
    sums = tuple(
        from_tiles(gathered[:, i * depth : (i + 1) * depth], part.shape)
        for i, part in enumerate(parts)
    )
    return sums, arrived[:, pieces.shape[1] :].reshape(rider.shape)


def on_device(
    grid_feat,
    cotangent,
    trace_feat,
    trace_dest,
    query_weight,
    key_weight,
    value_weight,
    output_weight,
):
    tile_count = lax.axis_size("inline") * lax.axis_size("crosslin")
    trace_rows = trace_feat.shape[0]
    model_width = trace_feat.shape[1]
    capacity = 2 * trace_rows * TOP // tile_count
    chosen, counts = slot_table(trace_dest, tile_count, capacity)
    picker = chosen.astype(jnp.bfloat16).reshape(tile_count * capacity, trace_rows)
    flag = jnp.ones((trace_rows, 128), jnp.bfloat16)
    packed = jnp.concatenate([trace_feat, flag], axis=1)
    outgoing = jnp.dot(picker, packed, preferred_element_type=jnp.float32).astype(jnp.bfloat16)
    arrived = send_slots(outgoing)
    feat_tile = arrived[:, :model_width]
    live_slots = arrived[:, model_width] > 0.5
    key_tile = jnp.dot(feat_tile, key_weight, preferred_element_type=jnp.float32).astype(
        jnp.bfloat16
    )
    value_tile = jnp.dot(feat_tile, value_weight, preferred_element_type=jnp.float32).astype(
        jnp.bfloat16
    )
    queries = jnp.dot(grid_feat, query_weight, preferred_element_type=jnp.float32).astype(
        jnp.bfloat16
    )
    out_grad = jnp.dot(cotangent, output_weight.T, preferred_element_type=jnp.float32).astype(
        jnp.bfloat16
    )
    attn_out, query_grad, key_grad, value_grad = fused_attention(
        queries, out_grad, key_tile, value_tile, live_slots
    )
    slot_trace = jnp.dot(key_grad, key_weight.T, preferred_element_type=jnp.float32)
    slot_trace = slot_trace + jnp.dot(
        value_grad, value_weight.T, preferred_element_type=jnp.float32
    )
    part_output = jnp.dot(attn_out.T, cotangent, preferred_element_type=jnp.float32)
    part_query = jnp.dot(grid_feat.T, query_grad, preferred_element_type=jnp.float32)
    part_key = jnp.dot(feat_tile.T, key_grad, preferred_element_type=jnp.float32)
    part_value = jnp.dot(feat_tile.T, value_grad, preferred_element_type=jnp.float32)
    (grad_query, grad_key, grad_value, grad_output), returned = sum_over_devices(
        (part_query, part_key, part_value, part_output), slot_trace.astype(jnp.bfloat16)
    )
    grad_grid = jnp.dot(query_grad, query_weight.T, preferred_element_type=jnp.float32).astype(
        jnp.bfloat16
    )
    grad_trace = jnp.dot(picker.T, returned, preferred_element_type=jnp.float32)
    return (grad_grid, grad_trace, grad_query, grad_key, grad_value, grad_output)


def solution(mesh):
    in_specs = (
        P(("inline", "crosslin"), None),
        P(("inline", "crosslin"), None),
        P(("inline", "crosslin"), None),
        P(("inline", "crosslin"), None),
        P(),
        P(),
        P(),
        P(),
    )
    out_specs = (
        P(("inline", "crosslin"), None),
        P(("inline", "crosslin"), None),
        P(),
        P(),
        P(),
        P(),
    )
    return jax.shard_map(
        on_device, mesh=mesh, in_specs=in_specs, out_specs=out_specs, check_vma=False
    )
```

```python
import jax
import jax.numpy as jnp
from jax import lax
from jax.experimental import pallas as pl
from jax.experimental.pallas import tpu as pltpu
from jax.sharding import PartitionSpec as P

HEADS = 8
TOP = 2


def slot_table(targets, tile_count, capacity):
    tile_ids = jnp.arange(tile_count, dtype=jnp.int32)
    named = jnp.any(targets[:, :, None] == tile_ids[None, None, :], axis=1)
    position = jnp.cumsum(named.astype(jnp.int32), axis=0) - 1
    places = jnp.arange(capacity, dtype=jnp.int32)
    chosen = named.T[:, None, :] & (position.T[:, None, :] == places[None, :, None])
    return (chosen, jnp.sum(named.astype(jnp.int32), axis=0))


def attention_kernel(
    q_ref, g_ref, k_ref, v_ref, live_ref, x_ref, c_ref,
    o_ref, dq_ref, dk_ref, dv_ref, po_ref, pq_ref, dk_acc, dv_acc,
):
    step = pl.program_id(0)
    width = q_ref.shape[1]
    head_size = width // HEADS
    factor = head_size ** (-0.5)

    @pl.when(step == 0)
    def _():
        dk_acc[...] = jnp.zeros_like(dk_acc)
        dv_acc[...] = jnp.zeros_like(dv_acc)
        po_ref[...] = jnp.zeros_like(po_ref)
        pq_ref[...] = jnp.zeros_like(pq_ref)

    live = live_ref[...] > 0.5
    for h in range(HEADS):
        cols = slice(h * head_size, (h + 1) * head_size)
        q_h = q_ref[:, cols]
        g_h = g_ref[:, cols]
        k_h = k_ref[:, cols]
        v_h = v_ref[:, cols]
        nt = (((1,), (1,)), ((), ()))
        tn = (((0,), (0,)), ((), ()))
        scores = lax.dot_general(q_h, k_h, nt, preferred_element_type=jnp.float32) * factor
        scores = jnp.where(live, scores, -1e30)
        peak = jnp.max(scores, axis=1, keepdims=True)
        raised = jnp.exp(scores - peak)
        attention = raised / jnp.sum(raised, axis=1, keepdims=True)
        prob_half = attention.astype(jnp.bfloat16)
        o_ref[:, cols] = jnp.dot(prob_half, v_h, preferred_element_type=jnp.float32).astype(o_ref.dtype)
        prob_grad = lax.dot_general(g_h, v_h, nt, preferred_element_type=jnp.float32)
        correction = jnp.sum(attention * prob_grad, axis=1, keepdims=True)
        score_grad = (attention * (prob_grad - correction) * factor).astype(jnp.bfloat16)
        dq_ref[:, cols] = jnp.dot(score_grad, k_h, preferred_element_type=jnp.float32).astype(dq_ref.dtype)
        dk_acc[:, cols] += lax.dot_general(score_grad, q_h, tn, preferred_element_type=jnp.float32)
        dv_acc[:, cols] += lax.dot_general(prob_half, g_h, tn, preferred_element_type=jnp.float32)

    tn = (((0,), (0,)), ((), ()))
    po_ref[...] += lax.dot_general(o_ref[...], c_ref[...], tn, preferred_element_type=jnp.float32)
    pq_ref[...] += lax.dot_general(x_ref[...], dq_ref[...], tn, preferred_element_type=jnp.float32)

    @pl.when(step == pl.num_programs(0) - 1)
    def _():
        dk_ref[...] = dk_acc[...].astype(dk_ref.dtype)
        dv_ref[...] = dv_acc[...].astype(dv_ref.dtype)


def fused_attention(queries, out_grad, key_tile, value_tile, live, grid_rows, upstream, block=512):
    rows, width = queries.shape
    slots = key_tile.shape[0]
    row_block = pl.BlockSpec((block, width), lambda i: (i, 0))
    slot_block = pl.BlockSpec((slots, width), lambda i: (0, 0))
    live_block = pl.BlockSpec((1, slots), lambda i: (0, 0))
    return pl.pallas_call(
        attention_kernel,
        grid=(rows // block,),
        in_specs=[row_block, row_block, slot_block, slot_block, live_block, row_block, row_block],
        out_specs=[row_block, row_block, slot_block, slot_block, slot_block, slot_block],
        out_shape=[
            jax.ShapeDtypeStruct((rows, width), jnp.bfloat16),
            jax.ShapeDtypeStruct((rows, width), jnp.bfloat16),
            jax.ShapeDtypeStruct((slots, width), jnp.bfloat16),
            jax.ShapeDtypeStruct((slots, width), jnp.bfloat16),
            jax.ShapeDtypeStruct((width, width), jnp.float32),
            jax.ShapeDtypeStruct((width, width), jnp.float32),
        ],
        scratch_shapes=[pltpu.VMEM((slots, width), jnp.float32), pltpu.VMEM((slots, width), jnp.float32)],
        compiler_params=pltpu.CompilerParams(dimension_semantics=("arbitrary",)),
    )(
        queries, out_grad, key_tile, value_tile, live.astype(jnp.float32).reshape(1, slots),
        grid_rows, upstream,
    )


def send_slots(outgoing):
    arrived = lax.all_to_all(
        outgoing, ("inline", "crosslin"), split_axis=0, concat_axis=0, tiled=True
    )
    return arrived


def as_tiles(part):
    rows, cols = part.shape
    return part.reshape(rows // 8, 8, cols // 128, 128).transpose(0, 2, 1, 3)


def from_tiles(tiles, shape):
    return tiles.reshape(shape[0] // 8, shape[1] // 128, 8, 128).transpose(0, 2, 1, 3).reshape(shape)


def sum_over_devices(parts, rider):
    count = lax.axis_size("inline") * lax.axis_size("crosslin")
    tiled = [as_tiles(part).reshape(count, -1, 128) for part in parts]
    depth = tiled[0].shape[1]
    pieces = jnp.concatenate(tiled, axis=1)
    mine = send_slots(pieces).sum(axis=0, keepdims=True).astype(jnp.bfloat16)
    rider_rows = rider.size // (count * 128)
    payload = jnp.concatenate(
        [jnp.broadcast_to(mine, pieces.shape), rider.reshape(count, rider_rows, 128)], axis=1
    )
    arrived = send_slots(payload)
    gathered = arrived[:, : pieces.shape[1]].astype(jnp.float32)
    sums = tuple(
        from_tiles(gathered[:, i * depth : (i + 1) * depth], part.shape)
        for i, part in enumerate(parts)
    )
    return sums, arrived[:, pieces.shape[1] :].reshape(rider.shape)


def on_device(
    grid_feat,
    cotangent,
    trace_feat,
    trace_dest,
    query_weight,
    key_weight,
    value_weight,
    output_weight,
):
    tile_count = lax.axis_size("inline") * lax.axis_size("crosslin")
    trace_rows = trace_feat.shape[0]
    model_width = trace_feat.shape[1]
    capacity = 2 * trace_rows * TOP // tile_count
    chosen, counts = slot_table(trace_dest, tile_count, capacity)
    picker = chosen.astype(jnp.bfloat16).reshape(tile_count * capacity, trace_rows)
    flag = jnp.ones((trace_rows, 128), jnp.bfloat16)
    packed = jnp.concatenate([trace_feat, flag], axis=1)
    outgoing = jnp.dot(picker, packed, preferred_element_type=jnp.float32).astype(jnp.bfloat16)
    arrived = send_slots(outgoing)
    feat_tile = arrived[:, :model_width]
    live_slots = arrived[:, model_width] > 0.5
    key_tile = jnp.dot(feat_tile, key_weight, preferred_element_type=jnp.float32).astype(
        jnp.bfloat16
    )
    value_tile = jnp.dot(feat_tile, value_weight, preferred_element_type=jnp.float32).astype(
        jnp.bfloat16
    )
    queries = jnp.dot(grid_feat, query_weight, preferred_element_type=jnp.float32).astype(
        jnp.bfloat16
    )
    out_grad = jnp.dot(cotangent, output_weight.T, preferred_element_type=jnp.float32).astype(
        jnp.bfloat16
    )
    attn_out, query_grad, key_grad, value_grad, part_output, part_query = fused_attention(
        queries, out_grad, key_tile, value_tile, live_slots, grid_feat, cotangent
    )
    slot_trace = jnp.dot(key_grad, key_weight.T, preferred_element_type=jnp.float32)
    slot_trace = slot_trace + jnp.dot(
        value_grad, value_weight.T, preferred_element_type=jnp.float32
    )
    part_key = jnp.dot(feat_tile.T, key_grad, preferred_element_type=jnp.float32)
    part_value = jnp.dot(feat_tile.T, value_grad, preferred_element_type=jnp.float32)
    (grad_query, grad_key, grad_value, grad_output), returned = sum_over_devices(
        (part_query, part_key, part_value, part_output), slot_trace.astype(jnp.bfloat16)
    )
    grad_grid = jnp.dot(query_grad, query_weight.T, preferred_element_type=jnp.float32).astype(
        jnp.bfloat16
    )
    grad_trace = jnp.dot(picker.T, returned, preferred_element_type=jnp.float32)
    return (grad_grid, grad_trace, grad_query, grad_key, grad_value, grad_output)


def solution(mesh):
    in_specs = (
        P(("inline", "crosslin"), None),
        P(("inline", "crosslin"), None),
        P(("inline", "crosslin"), None),
        P(("inline", "crosslin"), None),
        P(),
        P(),
        P(),
        P(),
    )
    out_specs = (
        P(("inline", "crosslin"), None),
        P(("inline", "crosslin"), None),
        P(),
        P(),
        P(),
        P(),
    )
    return jax.shard_map(
        on_device, mesh=mesh, in_specs=in_specs, out_specs=out_specs, check_vma=False
    )
```

```python
import jax
import jax.numpy as jnp
from jax import lax
from jax.experimental import pallas as pl
from jax.experimental.pallas import tpu as pltpu
from jax.sharding import PartitionSpec as P

HEADS = 8
TOP = 2


def slot_table(targets, tile_count, capacity):
    tile_ids = jnp.arange(tile_count, dtype=jnp.int32)
    named = jnp.any(targets[:, :, None] == tile_ids[None, None, :], axis=1)
    position = jnp.cumsum(named.astype(jnp.int32), axis=0) - 1
    places = jnp.arange(capacity, dtype=jnp.int32)
    chosen = named.T[:, None, :] & (position.T[:, None, :] == places[None, :, None])
    return (chosen, jnp.sum(named.astype(jnp.int32), axis=0))


def attention_kernel(
    q_ref, g_ref, f_ref, wk_ref, wv_ref, live_ref, x_ref, c_ref,
    o_ref, dq_ref, dk_ref, dv_ref, po_ref, pq_ref, pk_ref, pv_ref, k_ref, v_ref, dk_acc, dv_acc,
):
    step = pl.program_id(0)
    width = q_ref.shape[1]
    head_size = width // HEADS
    factor = head_size ** (-0.5)

    @pl.when(step == 0)
    def _():
        dk_acc[...] = jnp.zeros_like(dk_acc)
        dv_acc[...] = jnp.zeros_like(dv_acc)
        po_ref[...] = jnp.zeros_like(po_ref)
        pq_ref[...] = jnp.zeros_like(pq_ref)
        feat = f_ref[...]
        k_ref[...] = jnp.dot(feat, wk_ref[...], preferred_element_type=jnp.float32).astype(k_ref.dtype)
        v_ref[...] = jnp.dot(feat, wv_ref[...], preferred_element_type=jnp.float32).astype(v_ref.dtype)

    live = live_ref[...] > 0.5
    for h in range(HEADS):
        cols = slice(h * head_size, (h + 1) * head_size)
        q_h = q_ref[:, cols]
        g_h = g_ref[:, cols]
        k_h = k_ref[:, cols]
        v_h = v_ref[:, cols]
        nt = (((1,), (1,)), ((), ()))
        tn = (((0,), (0,)), ((), ()))
        scores = lax.dot_general(q_h, k_h, nt, preferred_element_type=jnp.float32) * factor
        scores = jnp.where(live, scores, -1e30)
        peak = jnp.max(scores, axis=1, keepdims=True)
        raised = jnp.exp(scores - peak)
        attention = raised / jnp.sum(raised, axis=1, keepdims=True)
        prob_half = attention.astype(jnp.bfloat16)
        o_ref[:, cols] = jnp.dot(prob_half, v_h, preferred_element_type=jnp.float32).astype(o_ref.dtype)
        prob_grad = lax.dot_general(g_h, v_h, nt, preferred_element_type=jnp.float32)
        correction = jnp.sum(attention * prob_grad, axis=1, keepdims=True)
        score_grad = (attention * (prob_grad - correction) * factor).astype(jnp.bfloat16)
        dq_ref[:, cols] = jnp.dot(score_grad, k_h, preferred_element_type=jnp.float32).astype(dq_ref.dtype)
        dk_acc[:, cols] += lax.dot_general(score_grad, q_h, tn, preferred_element_type=jnp.float32)
        dv_acc[:, cols] += lax.dot_general(prob_half, g_h, tn, preferred_element_type=jnp.float32)

    tn = (((0,), (0,)), ((), ()))
    po_ref[...] += lax.dot_general(o_ref[...], c_ref[...], tn, preferred_element_type=jnp.float32)
    pq_ref[...] += lax.dot_general(x_ref[...], dq_ref[...], tn, preferred_element_type=jnp.float32)

    @pl.when(step == pl.num_programs(0) - 1)
    def _():
        key_grad = dk_acc[...].astype(dk_ref.dtype)
        value_grad = dv_acc[...].astype(dv_ref.dtype)
        dk_ref[...] = key_grad
        dv_ref[...] = value_grad
        pk_ref[...] = lax.dot_general(f_ref[...], key_grad, tn, preferred_element_type=jnp.float32)
        pv_ref[...] = lax.dot_general(f_ref[...], value_grad, tn, preferred_element_type=jnp.float32)


def fused_attention(
    queries, out_grad, feat_tile, key_weight, value_weight, live, grid_rows, upstream, block=512
):
    rows, width = queries.shape
    slots = feat_tile.shape[0]
    row_block = pl.BlockSpec((block, width), lambda i: (i, 0))
    slot_block = pl.BlockSpec((slots, width), lambda i: (0, 0))
    live_block = pl.BlockSpec((1, slots), lambda i: (0, 0))
    weight_block = pl.BlockSpec((width, width), lambda i: (0, 0))
    return pl.pallas_call(
        attention_kernel,
        grid=(rows // block,),
        in_specs=[
            row_block, row_block, slot_block, weight_block, weight_block, live_block,
            row_block, row_block,
        ],
        out_specs=[
            row_block, row_block, slot_block, slot_block,
            weight_block, weight_block, weight_block, weight_block,
        ],
        out_shape=[
            jax.ShapeDtypeStruct((rows, width), jnp.bfloat16),
            jax.ShapeDtypeStruct((rows, width), jnp.bfloat16),
            jax.ShapeDtypeStruct((slots, width), jnp.bfloat16),
            jax.ShapeDtypeStruct((slots, width), jnp.bfloat16),
            jax.ShapeDtypeStruct((width, width), jnp.float32),
            jax.ShapeDtypeStruct((width, width), jnp.float32),
            jax.ShapeDtypeStruct((width, width), jnp.float32),
            jax.ShapeDtypeStruct((width, width), jnp.float32),
        ],
        scratch_shapes=[
            pltpu.VMEM((slots, width), jnp.bfloat16),
            pltpu.VMEM((slots, width), jnp.bfloat16),
            pltpu.VMEM((slots, width), jnp.float32),
            pltpu.VMEM((slots, width), jnp.float32),
        ],
        compiler_params=pltpu.CompilerParams(dimension_semantics=("arbitrary",)),
    )(
        queries, out_grad, feat_tile, key_weight, value_weight,
        live.astype(jnp.float32).reshape(1, slots), grid_rows, upstream,
    )


def send_slots(outgoing):
    arrived = lax.all_to_all(
        outgoing, ("inline", "crosslin"), split_axis=0, concat_axis=0, tiled=True
    )
    return arrived


def as_tiles(part):
    rows, cols = part.shape
    return part.reshape(rows // 8, 8, cols // 128, 128).transpose(0, 2, 1, 3)


def from_tiles(tiles, shape):
    return tiles.reshape(shape[0] // 8, shape[1] // 128, 8, 128).transpose(0, 2, 1, 3).reshape(shape)


def sum_over_devices(parts, rider):
    count = lax.axis_size("inline") * lax.axis_size("crosslin")
    tiled = [as_tiles(part).reshape(count, -1, 128) for part in parts]
    depth = tiled[0].shape[1]
    pieces = jnp.concatenate(tiled, axis=1)
    mine = send_slots(pieces).sum(axis=0, keepdims=True).astype(jnp.bfloat16)
    rider_rows = rider.size // (count * 128)
    payload = jnp.concatenate(
        [jnp.broadcast_to(mine, pieces.shape), rider.reshape(count, rider_rows, 128)], axis=1
    )
    arrived = send_slots(payload)
    gathered = arrived[:, : pieces.shape[1]].astype(jnp.float32)
    sums = tuple(
        from_tiles(gathered[:, i * depth : (i + 1) * depth], part.shape)
        for i, part in enumerate(parts)
    )
    return sums, arrived[:, pieces.shape[1] :].reshape(rider.shape)


def on_device(
    grid_feat,
    cotangent,
    trace_feat,
    trace_dest,
    query_weight,
    key_weight,
    value_weight,
    output_weight,
):
    tile_count = lax.axis_size("inline") * lax.axis_size("crosslin")
    trace_rows = trace_feat.shape[0]
    model_width = trace_feat.shape[1]
    capacity = 2 * trace_rows * TOP // tile_count
    chosen, counts = slot_table(trace_dest, tile_count, capacity)
    picker = chosen.astype(jnp.bfloat16).reshape(tile_count * capacity, trace_rows)
    flag = jnp.ones((trace_rows, 128), jnp.bfloat16)
    packed = jnp.concatenate([trace_feat, flag], axis=1)
    outgoing = jnp.dot(picker, packed, preferred_element_type=jnp.float32).astype(jnp.bfloat16)
    arrived = send_slots(outgoing)
    feat_tile = arrived[:, :model_width]
    live_slots = arrived[:, model_width] > 0.5
    queries = jnp.dot(grid_feat, query_weight, preferred_element_type=jnp.float32).astype(
        jnp.bfloat16
    )
    out_grad = jnp.dot(cotangent, output_weight.T, preferred_element_type=jnp.float32).astype(
        jnp.bfloat16
    )
    outs = fused_attention(
        queries, out_grad, feat_tile, key_weight, value_weight, live_slots, grid_feat, cotangent
    )
    attn_out, query_grad, key_grad, value_grad, part_output, part_query, part_key, part_value = outs
    slot_trace = jnp.dot(key_grad, key_weight.T, preferred_element_type=jnp.float32)
    slot_trace = slot_trace + jnp.dot(
        value_grad, value_weight.T, preferred_element_type=jnp.float32
    )
    (grad_query, grad_key, grad_value, grad_output), returned = sum_over_devices(
        (part_query, part_key, part_value, part_output), slot_trace.astype(jnp.bfloat16)
    )
    grad_grid = jnp.dot(query_grad, query_weight.T, preferred_element_type=jnp.float32).astype(
        jnp.bfloat16
    )
    grad_trace = jnp.dot(picker.T, returned, preferred_element_type=jnp.float32)
    return (grad_grid, grad_trace, grad_query, grad_key, grad_value, grad_output)


def solution(mesh):
    in_specs = (
        P(("inline", "crosslin"), None),
        P(("inline", "crosslin"), None),
        P(("inline", "crosslin"), None),
        P(("inline", "crosslin"), None),
        P(),
        P(),
        P(),
        P(),
    )
    out_specs = (
        P(("inline", "crosslin"), None),
        P(("inline", "crosslin"), None),
        P(),
        P(),
        P(),
        P(),
    )
    return jax.shard_map(
        on_device, mesh=mesh, in_specs=in_specs, out_specs=out_specs, check_vma=False
    )
```

```python
import jax
import jax.numpy as jnp
from jax import lax
from jax.experimental import pallas as pl
from jax.experimental.pallas import tpu as pltpu
from jax.sharding import PartitionSpec as P

HEADS = 8
TOP = 2


def slot_table(targets, tile_count, capacity):
    tile_ids = jnp.arange(tile_count, dtype=jnp.int32)
    named = jnp.any(targets[:, :, None] == tile_ids[None, None, :], axis=1)
    position = jnp.cumsum(named.astype(jnp.int32), axis=0) - 1
    places = jnp.arange(capacity, dtype=jnp.int32)
    chosen = named.T[:, None, :] & (position.T[:, None, :] == places[None, :, None])
    return (chosen, jnp.sum(named.astype(jnp.int32), axis=0))


def attention_kernel(
    q_ref, g_ref, f_ref, wk_ref, wv_ref, live_ref, x_ref, c_ref,
    o_ref, dq_ref, dk_ref, dv_ref, pieces_ref,
    k_ref, v_ref, dk_acc, dv_acc, pq_ref, pk_ref, pv_ref, po_ref,
):
    step = pl.program_id(0)
    width = q_ref.shape[1]
    head_size = width // HEADS
    factor = head_size ** (-0.5)

    @pl.when(step == 0)
    def _():
        dk_acc[...] = jnp.zeros_like(dk_acc)
        dv_acc[...] = jnp.zeros_like(dv_acc)
        po_ref[...] = jnp.zeros_like(po_ref)
        pq_ref[...] = jnp.zeros_like(pq_ref)
        feat = f_ref[...]
        k_ref[...] = jnp.dot(feat, wk_ref[...], preferred_element_type=jnp.float32).astype(k_ref.dtype)
        v_ref[...] = jnp.dot(feat, wv_ref[...], preferred_element_type=jnp.float32).astype(v_ref.dtype)

    live = live_ref[...] > 0.5
    for h in range(HEADS):
        cols = slice(h * head_size, (h + 1) * head_size)
        q_h = q_ref[:, cols]
        g_h = g_ref[:, cols]
        k_h = k_ref[:, cols]
        v_h = v_ref[:, cols]
        nt = (((1,), (1,)), ((), ()))
        tn = (((0,), (0,)), ((), ()))
        scores = lax.dot_general(q_h, k_h, nt, preferred_element_type=jnp.float32) * factor
        scores = jnp.where(live, scores, -1e30)
        peak = jnp.max(scores, axis=1, keepdims=True)
        raised = jnp.exp(scores - peak)
        attention = raised / jnp.sum(raised, axis=1, keepdims=True)
        prob_half = attention.astype(jnp.bfloat16)
        o_ref[:, cols] = jnp.dot(prob_half, v_h, preferred_element_type=jnp.float32).astype(o_ref.dtype)
        prob_grad = lax.dot_general(g_h, v_h, nt, preferred_element_type=jnp.float32)
        correction = jnp.sum(attention * prob_grad, axis=1, keepdims=True)
        score_grad = (attention * (prob_grad - correction) * factor).astype(jnp.bfloat16)
        dq_ref[:, cols] = jnp.dot(score_grad, k_h, preferred_element_type=jnp.float32).astype(dq_ref.dtype)
        dk_acc[:, cols] += lax.dot_general(score_grad, q_h, tn, preferred_element_type=jnp.float32)
        dv_acc[:, cols] += lax.dot_general(prob_half, g_h, tn, preferred_element_type=jnp.float32)

    tn = (((0,), (0,)), ((), ()))
    po_ref[...] += lax.dot_general(o_ref[...], c_ref[...], tn, preferred_element_type=jnp.float32)
    pq_ref[...] += lax.dot_general(x_ref[...], dq_ref[...], tn, preferred_element_type=jnp.float32)

    @pl.when(step == pl.num_programs(0) - 1)
    def _():
        key_grad = dk_acc[...].astype(dk_ref.dtype)
        value_grad = dv_acc[...].astype(dv_ref.dtype)
        dk_ref[...] = key_grad
        dv_ref[...] = value_grad
        pk_ref[...] = lax.dot_general(f_ref[...], key_grad, tn, preferred_element_type=jnp.float32)
        pv_ref[...] = lax.dot_general(f_ref[...], value_grad, tn, preferred_element_type=jnp.float32)
        parts = (pq_ref, pk_ref, pv_ref, po_ref)
        col_tiles = width // 128
        per_device = (width // 8) * col_tiles // pieces_ref.shape[0]
        depth = 8 * per_device

        def scatter_row(r, carry):
            for c in range(col_tiles):
                tile = r * col_tiles + c
                for i, part in enumerate(parts):
                    pieces_ref[tile // per_device, pl.ds(i * depth + (c % per_device) * 8, 8), :] = (
                        part[pl.ds(r * 8, 8), pl.ds(c * 128, 128)]
                    )
            return carry

        lax.fori_loop(0, width // 8, scatter_row, 0)


def fused_attention(
    queries, out_grad, feat_tile, key_weight, value_weight, live, grid_rows, upstream, count, block=512
):
    rows, width = queries.shape
    slots = feat_tile.shape[0]
    row_block = pl.BlockSpec((block, width), lambda i: (i, 0))
    slot_block = pl.BlockSpec((slots, width), lambda i: (0, 0))
    live_block = pl.BlockSpec((1, slots), lambda i: (0, 0))
    weight_block = pl.BlockSpec((width, width), lambda i: (0, 0))
    depth = 4 * width * width // (count * 128)
    return pl.pallas_call(
        attention_kernel,
        grid=(rows // block,),
        in_specs=[
            row_block, row_block, slot_block, weight_block, weight_block, live_block,
            row_block, row_block,
        ],
        out_specs=[
            row_block, row_block, slot_block, slot_block,
            pl.BlockSpec((count, depth, 128), lambda i: (0, 0, 0)),
        ],
        out_shape=[
            jax.ShapeDtypeStruct((rows, width), jnp.bfloat16),
            jax.ShapeDtypeStruct((rows, width), jnp.bfloat16),
            jax.ShapeDtypeStruct((slots, width), jnp.bfloat16),
            jax.ShapeDtypeStruct((slots, width), jnp.bfloat16),
            jax.ShapeDtypeStruct((count, depth, 128), jnp.float32),
        ],
        scratch_shapes=[
            pltpu.VMEM((slots, width), jnp.bfloat16),
            pltpu.VMEM((slots, width), jnp.bfloat16),
            pltpu.VMEM((slots, width), jnp.float32),
            pltpu.VMEM((slots, width), jnp.float32),
            pltpu.VMEM((width, width), jnp.float32),
            pltpu.VMEM((width, width), jnp.float32),
            pltpu.VMEM((width, width), jnp.float32),
            pltpu.VMEM((width, width), jnp.float32),
        ],
        compiler_params=pltpu.CompilerParams(dimension_semantics=("arbitrary",)),
    )(
        queries, out_grad, feat_tile, key_weight, value_weight,
        live.astype(jnp.float32).reshape(1, slots), grid_rows, upstream,
    )


def send_slots(outgoing):
    arrived = lax.all_to_all(
        outgoing, ("inline", "crosslin"), split_axis=0, concat_axis=0, tiled=True
    )
    return arrived


def from_tiles(tiles, shape):
    return tiles.reshape(shape[0] // 8, shape[1] // 128, 8, 128).transpose(0, 2, 1, 3).reshape(shape)


def sum_over_devices(pieces, shape, rider):
    count = pieces.shape[0]
    depth = pieces.shape[1] // 4
    mine = send_slots(pieces).sum(axis=0, keepdims=True).astype(jnp.bfloat16)
    rider_rows = rider.size // (count * 128)
    payload = jnp.concatenate(
        [jnp.broadcast_to(mine, pieces.shape), rider.reshape(count, rider_rows, 128)], axis=1
    )
    arrived = send_slots(payload)
    gathered = arrived[:, : pieces.shape[1]].astype(jnp.float32)
    sums = tuple(from_tiles(gathered[:, i * depth : (i + 1) * depth], shape) for i in range(4))
    return sums, arrived[:, pieces.shape[1] :].reshape(rider.shape)


def on_device(
    grid_feat,
    cotangent,
    trace_feat,
    trace_dest,
    query_weight,
    key_weight,
    value_weight,
    output_weight,
):
    tile_count = lax.axis_size("inline") * lax.axis_size("crosslin")
    trace_rows = trace_feat.shape[0]
    model_width = trace_feat.shape[1]
    capacity = 2 * trace_rows * TOP // tile_count
    chosen, counts = slot_table(trace_dest, tile_count, capacity)
    picker = chosen.astype(jnp.bfloat16).reshape(tile_count * capacity, trace_rows)
    flag = jnp.ones((trace_rows, 128), jnp.bfloat16)
    packed = jnp.concatenate([trace_feat, flag], axis=1)
    outgoing = jnp.dot(picker, packed, preferred_element_type=jnp.float32).astype(jnp.bfloat16)
    arrived = send_slots(outgoing)
    feat_tile = arrived[:, :model_width]
    live_slots = arrived[:, model_width] > 0.5
    queries = jnp.dot(grid_feat, query_weight, preferred_element_type=jnp.float32).astype(
        jnp.bfloat16
    )
    out_grad = jnp.dot(cotangent, output_weight.T, preferred_element_type=jnp.float32).astype(
        jnp.bfloat16
    )
    attn_out, query_grad, key_grad, value_grad, pieces = fused_attention(
        queries, out_grad, feat_tile, key_weight, value_weight, live_slots, grid_feat, cotangent,
        tile_count,
    )
    slot_trace = jnp.dot(key_grad, key_weight.T, preferred_element_type=jnp.float32)
    slot_trace = slot_trace + jnp.dot(
        value_grad, value_weight.T, preferred_element_type=jnp.float32
    )
    (grad_query, grad_key, grad_value, grad_output), returned = sum_over_devices(
        pieces, (model_width, model_width), slot_trace.astype(jnp.bfloat16)
    )
    grad_grid = jnp.dot(query_grad, query_weight.T, preferred_element_type=jnp.float32).astype(
        jnp.bfloat16
    )
    grad_trace = jnp.dot(picker.T, returned, preferred_element_type=jnp.float32)
    return (grad_grid, grad_trace, grad_query, grad_key, grad_value, grad_output)


def solution(mesh):
    in_specs = (
        P(("inline", "crosslin"), None),
        P(("inline", "crosslin"), None),
        P(("inline", "crosslin"), None),
        P(("inline", "crosslin"), None),
        P(),
        P(),
        P(),
        P(),
    )
    out_specs = (
        P(("inline", "crosslin"), None),
        P(("inline", "crosslin"), None),
        P(),
        P(),
        P(),
        P(),
    )
    return jax.shard_map(
        on_device, mesh=mesh, in_specs=in_specs, out_specs=out_specs, check_vma=False
    )
```

```python
import jax
import jax.numpy as jnp
from jax import lax
from jax.experimental import pallas as pl
from jax.experimental.pallas import tpu as pltpu
from jax.sharding import PartitionSpec as P

HEADS = 8
TOP = 2


def slot_table(targets, tile_count, capacity):
    tile_ids = jnp.arange(tile_count, dtype=jnp.int32)
    named = jnp.any(targets[:, :, None] == tile_ids[None, None, :], axis=1)
    position = jnp.cumsum(named.astype(jnp.int32), axis=0) - 1
    places = jnp.arange(capacity, dtype=jnp.int32)
    chosen = named.T[:, None, :] & (position.T[:, None, :] == places[None, :, None])
    return (chosen, jnp.sum(named.astype(jnp.int32), axis=0))


def attention_kernel(
    q_ref, g_ref, f_ref, wk_ref, wv_ref, live_ref, x_ref, c_ref,
    o_ref, dq_ref, dk_ref, dv_ref, pieces_ref,
    k_ref, v_ref, dk_acc, dv_acc, pq_ref, pk_ref, pv_ref, po_ref,
):
    step = pl.program_id(0)
    width = q_ref.shape[1]
    head_size = width // HEADS
    factor = head_size ** (-0.5)

    @pl.when(step == 0)
    def _():
        dk_acc[...] = jnp.zeros_like(dk_acc)
        dv_acc[...] = jnp.zeros_like(dv_acc)
        po_ref[...] = jnp.zeros_like(po_ref)
        pq_ref[...] = jnp.zeros_like(pq_ref)
        feat = f_ref[...]
        k_ref[...] = jnp.dot(feat, wk_ref[...], preferred_element_type=jnp.float32).astype(k_ref.dtype)
        v_ref[...] = jnp.dot(feat, wv_ref[...], preferred_element_type=jnp.float32).astype(v_ref.dtype)

    live = live_ref[...] > 0.5
    for h in range(HEADS):
        cols = slice(h * head_size, (h + 1) * head_size)
        q_h = q_ref[:, cols]
        g_h = g_ref[:, cols]
        k_h = k_ref[:, cols]
        v_h = v_ref[:, cols]
        nt = (((1,), (1,)), ((), ()))
        tn = (((0,), (0,)), ((), ()))
        scores = lax.dot_general(q_h, k_h, nt, preferred_element_type=jnp.float32) * factor
        scores = jnp.where(live, scores, -1e30)
        peak = jnp.max(scores, axis=1, keepdims=True)
        raised = jnp.exp(scores - peak)
        attention = raised / jnp.sum(raised, axis=1, keepdims=True)
        prob_half = attention.astype(jnp.bfloat16)
        o_ref[:, cols] = jnp.dot(prob_half, v_h, preferred_element_type=jnp.float32).astype(o_ref.dtype)
        prob_grad = lax.dot_general(g_h, v_h, nt, preferred_element_type=jnp.float32)
        correction = jnp.sum(attention * prob_grad, axis=1, keepdims=True)
        score_grad = (attention * (prob_grad - correction) * factor).astype(jnp.bfloat16)
        dq_ref[:, cols] = jnp.dot(score_grad, k_h, preferred_element_type=jnp.float32).astype(dq_ref.dtype)
        dk_acc[:, cols] += lax.dot_general(score_grad, q_h, tn, preferred_element_type=jnp.float32)
        dv_acc[:, cols] += lax.dot_general(prob_half, g_h, tn, preferred_element_type=jnp.float32)

    tn = (((0,), (0,)), ((), ()))
    po_ref[...] += lax.dot_general(o_ref[...], c_ref[...], tn, preferred_element_type=jnp.float32)
    pq_ref[...] += lax.dot_general(x_ref[...], dq_ref[...], tn, preferred_element_type=jnp.float32)

    @pl.when(step == pl.num_programs(0) - 1)
    def _():
        key_grad = dk_acc[...].astype(dk_ref.dtype)
        value_grad = dv_acc[...].astype(dv_ref.dtype)
        dk_ref[...] = key_grad
        dv_ref[...] = value_grad
        pk_ref[...] = lax.dot_general(f_ref[...], key_grad, tn, preferred_element_type=jnp.float32)
        pv_ref[...] = lax.dot_general(f_ref[...], value_grad, tn, preferred_element_type=jnp.float32)
        parts = (pq_ref, pk_ref, pv_ref, po_ref)
        col_tiles = width // 128
        per_device = (width // 8) * col_tiles // pieces_ref.shape[0]
        depth = 8 * per_device

        def scatter_row(r, carry):
            for c in range(col_tiles):
                tile = r * col_tiles + c
                for i, part in enumerate(parts):
                    pieces_ref[tile // per_device, pl.ds(i * depth + (c % per_device) * 8, 8), :] = (
                        part[pl.ds(r * 8, 8), pl.ds(c * 128, 128)]
                    )
            return carry

        lax.fori_loop(0, width // 8, scatter_row, 0)


def fused_attention(
    queries, out_grad, feat_tile, key_weight, value_weight, live, grid_rows, upstream, count, block=1024
):
    rows, width = queries.shape
    slots = feat_tile.shape[0]
    row_block = pl.BlockSpec((block, width), lambda i: (i, 0))
    slot_block = pl.BlockSpec((slots, width), lambda i: (0, 0))
    live_block = pl.BlockSpec((1, slots), lambda i: (0, 0))
    weight_block = pl.BlockSpec((width, width), lambda i: (0, 0))
    depth = 4 * width * width // (count * 128)
    return pl.pallas_call(
        attention_kernel,
        grid=(rows // block,),
        in_specs=[
            row_block, row_block, slot_block, weight_block, weight_block, live_block,
            row_block, row_block,
        ],
        out_specs=[
            row_block, row_block, slot_block, slot_block,
            pl.BlockSpec((count, depth, 128), lambda i: (0, 0, 0)),
        ],
        out_shape=[
            jax.ShapeDtypeStruct((rows, width), jnp.bfloat16),
            jax.ShapeDtypeStruct((rows, width), jnp.bfloat16),
            jax.ShapeDtypeStruct((slots, width), jnp.bfloat16),
            jax.ShapeDtypeStruct((slots, width), jnp.bfloat16),
            jax.ShapeDtypeStruct((count, depth, 128), jnp.float32),
        ],
        scratch_shapes=[
            pltpu.VMEM((slots, width), jnp.bfloat16),
            pltpu.VMEM((slots, width), jnp.bfloat16),
            pltpu.VMEM((slots, width), jnp.float32),
            pltpu.VMEM((slots, width), jnp.float32),
            pltpu.VMEM((width, width), jnp.float32),
            pltpu.VMEM((width, width), jnp.float32),
            pltpu.VMEM((width, width), jnp.float32),
            pltpu.VMEM((width, width), jnp.float32),
        ],
        compiler_params=pltpu.CompilerParams(dimension_semantics=("arbitrary",)),
    )(
        queries, out_grad, feat_tile, key_weight, value_weight,
        live.astype(jnp.float32).reshape(1, slots), grid_rows, upstream,
    )


def send_slots(outgoing):
    arrived = lax.all_to_all(
        outgoing, ("inline", "crosslin"), split_axis=0, concat_axis=0, tiled=True
    )
    return arrived


def from_tiles(tiles, shape):
    return tiles.reshape(shape[0] // 8, shape[1] // 128, 8, 128).transpose(0, 2, 1, 3).reshape(shape)


def sum_over_devices(pieces, shape, rider):
    count = pieces.shape[0]
    depth = pieces.shape[1] // 4
    mine = send_slots(pieces).sum(axis=0, keepdims=True).astype(jnp.bfloat16)
    rider_rows = rider.size // (count * 128)
    payload = jnp.concatenate(
        [jnp.broadcast_to(mine, pieces.shape), rider.reshape(count, rider_rows, 128)], axis=1
    )
    arrived = send_slots(payload)
    gathered = arrived[:, : pieces.shape[1]].astype(jnp.float32)
    sums = tuple(from_tiles(gathered[:, i * depth : (i + 1) * depth], shape) for i in range(4))
    return sums, arrived[:, pieces.shape[1] :].reshape(count * rider_rows, 128)


def on_device(
    grid_feat,
    cotangent,
    trace_feat,
    trace_dest,
    query_weight,
    key_weight,
    value_weight,
    output_weight,
):
    tile_count = lax.axis_size("inline") * lax.axis_size("crosslin")
    trace_rows = trace_feat.shape[0]
    model_width = trace_feat.shape[1]
    capacity = 2 * trace_rows * TOP // tile_count
    chosen, counts = slot_table(trace_dest, tile_count, capacity)
    picker = chosen.astype(jnp.bfloat16).reshape(tile_count * capacity, trace_rows)
    flag = jnp.ones((trace_rows, 128), jnp.bfloat16)
    packed = jnp.concatenate([trace_feat, flag], axis=1)
    outgoing = jnp.dot(picker, packed, preferred_element_type=jnp.float32).astype(jnp.bfloat16)
    arrived = send_slots(outgoing)
    feat_tile = arrived[:, :model_width]
    live_slots = arrived[:, model_width] > 0.5
    queries = jnp.dot(grid_feat, query_weight, preferred_element_type=jnp.float32).astype(
        jnp.bfloat16
    )
    out_grad = jnp.dot(cotangent, output_weight.T, preferred_element_type=jnp.float32).astype(
        jnp.bfloat16
    )
    attn_out, query_grad, key_grad, value_grad, pieces = fused_attention(
        queries, out_grad, feat_tile, key_weight, value_weight, live_slots, grid_feat, cotangent,
        tile_count,
    )
    slot_trace = jnp.dot(key_grad, key_weight.T, preferred_element_type=jnp.float32)
    slot_trace = slot_trace + jnp.dot(
        value_grad, value_weight.T, preferred_element_type=jnp.float32
    )
    (grad_query, grad_key, grad_value, grad_output), returned = sum_over_devices(
        pieces, (model_width, model_width), slot_trace.astype(jnp.bfloat16)
    )
    grad_grid = jnp.dot(query_grad, query_weight.T, preferred_element_type=jnp.float32).astype(
        jnp.bfloat16
    )
    col_blocks = model_width // 128
    spread = picker.reshape(tile_count * capacity, 1, 1, trace_rows) * jnp.eye(
        col_blocks, dtype=picker.dtype
    )[None, :, :, None]
    spread = spread.reshape(tile_count * capacity * col_blocks, col_blocks, trace_rows)
    grad_trace = jnp.einsum(
        "kcr,kl->rcl", spread, returned, preferred_element_type=jnp.float32
    ).reshape(trace_rows, model_width)
    return (grad_grid, grad_trace, grad_query, grad_key, grad_value, grad_output)


def solution(mesh):
    in_specs = (
        P(("inline", "crosslin"), None),
        P(("inline", "crosslin"), None),
        P(("inline", "crosslin"), None),
        P(("inline", "crosslin"), None),
        P(),
        P(),
        P(),
        P(),
    )
    out_specs = (
        P(("inline", "crosslin"), None),
        P(("inline", "crosslin"), None),
        P(),
        P(),
        P(),
        P(),
    )
    return jax.shard_map(
        on_device, mesh=mesh, in_specs=in_specs, out_specs=out_specs, check_vma=False
    )
```

```python
import jax
import jax.numpy as jnp
from jax import lax
from jax.experimental import pallas as pl
from jax.experimental.pallas import tpu as pltpu
from jax.sharding import PartitionSpec as P

HEADS = 8
TOP = 2


def slot_table(targets, tile_count, capacity):
    tile_ids = jnp.arange(tile_count, dtype=jnp.int32)
    named = jnp.any(targets[:, :, None] == tile_ids[None, None, :], axis=1)
    position = jnp.cumsum(named.astype(jnp.int32), axis=0) - 1
    places = jnp.arange(capacity, dtype=jnp.int32)
    chosen = named.T[:, None, :] & (position.T[:, None, :] == places[None, :, None])
    return (chosen, jnp.sum(named.astype(jnp.int32), axis=0))


def attention_kernel(
    q_ref, g_ref, f_ref, wk_ref, wv_ref, live_ref, x_ref, c_ref,
    o_ref, dq_ref, dk_ref, dv_ref, pieces_ref,
    k_ref, v_ref, dk_acc, dv_acc, pq_ref, pk_ref, pv_ref, po_ref,
):
    step = pl.program_id(0)
    width = q_ref.shape[1]
    head_size = width // HEADS
    factor = head_size ** (-0.5)

    @pl.when(step == 0)
    def _():
        dk_acc[...] = jnp.zeros_like(dk_acc)
        dv_acc[...] = jnp.zeros_like(dv_acc)
        po_ref[...] = jnp.zeros_like(po_ref)
        pq_ref[...] = jnp.zeros_like(pq_ref)
        feat = f_ref[...]
        k_ref[...] = jnp.dot(feat, wk_ref[...], preferred_element_type=jnp.float32).astype(k_ref.dtype)
        v_ref[...] = jnp.dot(feat, wv_ref[...], preferred_element_type=jnp.float32).astype(v_ref.dtype)

    live = live_ref[...] > 0.5
    for h in range(HEADS):
        cols = slice(h * head_size, (h + 1) * head_size)
        q_h = q_ref[:, cols]
        g_h = g_ref[:, cols]
        k_h = k_ref[:, cols]
        v_h = v_ref[:, cols]
        nt = (((1,), (1,)), ((), ()))
        tn = (((0,), (0,)), ((), ()))
        scores = lax.dot_general(q_h, k_h, nt, preferred_element_type=jnp.float32) * factor
        scores = jnp.where(live, scores, -1e30)
        peak = jnp.max(scores, axis=1, keepdims=True)
        raised = jnp.exp(scores - peak)
        attention = raised / jnp.sum(raised, axis=1, keepdims=True)
        prob_half = attention.astype(jnp.bfloat16)
        o_ref[:, cols] = jnp.dot(prob_half, v_h, preferred_element_type=jnp.float32).astype(o_ref.dtype)
        prob_grad = lax.dot_general(g_h, v_h, nt, preferred_element_type=jnp.float32)
        correction = jnp.sum(attention * prob_grad, axis=1, keepdims=True)
        score_grad = (attention * (prob_grad - correction) * factor).astype(jnp.bfloat16)
        dq_ref[:, cols] = jnp.dot(score_grad, k_h, preferred_element_type=jnp.float32).astype(dq_ref.dtype)
        dk_acc[:, cols] += lax.dot_general(score_grad, q_h, tn, preferred_element_type=jnp.float32)
        dv_acc[:, cols] += lax.dot_general(prob_half, g_h, tn, preferred_element_type=jnp.float32)

    tn = (((0,), (0,)), ((), ()))
    po_ref[...] += lax.dot_general(o_ref[...], c_ref[...], tn, preferred_element_type=jnp.float32)
    pq_ref[...] += lax.dot_general(x_ref[...], dq_ref[...], tn, preferred_element_type=jnp.float32)

    @pl.when(step == pl.num_programs(0) - 1)
    def _():
        key_grad = dk_acc[...].astype(dk_ref.dtype)
        value_grad = dv_acc[...].astype(dv_ref.dtype)
        dk_ref[...] = key_grad
        dv_ref[...] = value_grad
        pk_ref[...] = lax.dot_general(f_ref[...], key_grad, tn, preferred_element_type=jnp.float32)
        pv_ref[...] = lax.dot_general(f_ref[...], value_grad, tn, preferred_element_type=jnp.float32)
        parts = (pq_ref, pk_ref, pv_ref, po_ref)
        col_tiles = width // 128
        per_device = (width // 8) * col_tiles // pieces_ref.shape[0]
        depth = 8 * per_device

        def scatter_row(r, carry):
            for c in range(col_tiles):
                tile = r * col_tiles + c
                for i, part in enumerate(parts):
                    pieces_ref[tile // per_device, pl.ds(i * depth + (c % per_device) * 8, 8), :] = (
                        part[pl.ds(r * 8, 8), pl.ds(c * 128, 128)]
                    )
            return carry

        lax.fori_loop(0, width // 8, scatter_row, 0)


def fused_attention(
    queries, out_grad, feat_tile, key_weight, value_weight, live, grid_rows, upstream, count, block=512
):
    rows, width = queries.shape
    slots = feat_tile.shape[0]
    row_block = pl.BlockSpec((block, width), lambda i: (i, 0))
    slot_block = pl.BlockSpec((slots, width), lambda i: (0, 0))
    live_block = pl.BlockSpec((1, slots), lambda i: (0, 0))
    weight_block = pl.BlockSpec((width, width), lambda i: (0, 0))
    depth = 4 * width * width // (count * 128)
    return pl.pallas_call(
        attention_kernel,
        grid=(rows // block,),
        in_specs=[
            row_block, row_block, slot_block, weight_block, weight_block, live_block,
            row_block, row_block,
        ],
        out_specs=[
            row_block, row_block, slot_block, slot_block,
            pl.BlockSpec((count, depth, 128), lambda i: (0, 0, 0)),
        ],
        out_shape=[
            jax.ShapeDtypeStruct((rows, width), jnp.bfloat16),
            jax.ShapeDtypeStruct((rows, width), jnp.bfloat16),
            jax.ShapeDtypeStruct((slots, width), jnp.bfloat16),
            jax.ShapeDtypeStruct((slots, width), jnp.bfloat16),
            jax.ShapeDtypeStruct((count, depth, 128), jnp.float32),
        ],
        scratch_shapes=[
            pltpu.VMEM((slots, width), jnp.bfloat16),
            pltpu.VMEM((slots, width), jnp.bfloat16),
            pltpu.VMEM((slots, width), jnp.float32),
            pltpu.VMEM((slots, width), jnp.float32),
            pltpu.VMEM((width, width), jnp.float32),
            pltpu.VMEM((width, width), jnp.float32),
            pltpu.VMEM((width, width), jnp.float32),
            pltpu.VMEM((width, width), jnp.float32),
        ],
        compiler_params=pltpu.CompilerParams(dimension_semantics=("arbitrary",)),
    )(
        queries, out_grad, feat_tile, key_weight, value_weight,
        live.astype(jnp.float32).reshape(1, slots), grid_rows, upstream,
    )


def send_slots(outgoing):
    arrived = lax.all_to_all(
        outgoing, ("inline", "crosslin"), split_axis=0, concat_axis=0, tiled=True
    )
    return arrived


def from_tiles(tiles, shape):
    return tiles.reshape(shape[0] // 8, shape[1] // 128, 8, 128).transpose(0, 2, 1, 3).reshape(shape)


def sum_over_devices(pieces, shape, rider):
    count = pieces.shape[0]
    depth = pieces.shape[1] // 4
    mine = send_slots(pieces).sum(axis=0, keepdims=True).astype(jnp.bfloat16)
    rider_rows = rider.size // (count * 128)
    payload = jnp.concatenate(
        [jnp.broadcast_to(mine, pieces.shape), rider.reshape(count, rider_rows, 128)], axis=1
    )
    arrived = send_slots(payload)
    gathered = arrived[:, : pieces.shape[1]].astype(jnp.float32)
    sums = tuple(from_tiles(gathered[:, i * depth : (i + 1) * depth], shape) for i in range(4))
    return sums, arrived[:, pieces.shape[1] :].reshape(count * rider_rows, 128)


def on_device(
    grid_feat,
    cotangent,
    trace_feat,
    trace_dest,
    query_weight,
    key_weight,
    value_weight,
    output_weight,
):
    tile_count = lax.axis_size("inline") * lax.axis_size("crosslin")
    trace_rows = trace_feat.shape[0]
    model_width = trace_feat.shape[1]
    capacity = 2 * trace_rows * TOP // tile_count
    chosen, counts = slot_table(trace_dest, tile_count, capacity)
    picker = chosen.astype(jnp.bfloat16).reshape(tile_count * capacity, trace_rows)
    flag = jnp.ones((trace_rows, 128), jnp.bfloat16)
    packed = jnp.concatenate([trace_feat, flag], axis=1)
    outgoing = jnp.dot(picker, packed, preferred_element_type=jnp.float32).astype(jnp.bfloat16)
    arrived = send_slots(outgoing)
    feat_tile = arrived[:, :model_width]
    live_slots = arrived[:, model_width] > 0.5
    queries = jnp.dot(grid_feat, query_weight, preferred_element_type=jnp.float32).astype(
        jnp.bfloat16
    )
    out_grad = jnp.dot(cotangent, output_weight.T, preferred_element_type=jnp.float32).astype(
        jnp.bfloat16
    )
    attn_out, query_grad, key_grad, value_grad, pieces = fused_attention(
        queries, out_grad, feat_tile, key_weight, value_weight, live_slots, grid_feat, cotangent,
        tile_count,
    )
    slot_trace = jnp.dot(key_grad, key_weight.T, preferred_element_type=jnp.float32)
    slot_trace = slot_trace + jnp.dot(
        value_grad, value_weight.T, preferred_element_type=jnp.float32
    )
    (grad_query, grad_key, grad_value, grad_output), returned = sum_over_devices(
        pieces, (model_width, model_width), slot_trace.astype(jnp.bfloat16)
    )
    grad_grid = jnp.dot(query_grad, query_weight.T, preferred_element_type=jnp.float32).astype(
        jnp.bfloat16
    )
    col_blocks = model_width // 128
    spread = picker.reshape(tile_count * capacity, 1, 1, trace_rows) * jnp.eye(
        col_blocks, dtype=picker.dtype
    )[None, :, :, None]
    spread = spread.reshape(tile_count * capacity * col_blocks, col_blocks, trace_rows)
    grad_trace = jnp.einsum(
        "kcr,kl->rcl", spread, returned, preferred_element_type=jnp.float32
    ).reshape(trace_rows, model_width)
    return (grad_grid, grad_trace, grad_query, grad_key, grad_value, grad_output)


def solution(mesh):
    in_specs = (
        P(("inline", "crosslin"), None),
        P(("inline", "crosslin"), None),
        P(("inline", "crosslin"), None),
        P(("inline", "crosslin"), None),
        P(),
        P(),
        P(),
        P(),
    )
    out_specs = (
        P(("inline", "crosslin"), None),
        P(("inline", "crosslin"), None),
        P(),
        P(),
        P(),
        P(),
    )
    return jax.shard_map(
        on_device, mesh=mesh, in_specs=in_specs, out_specs=out_specs, check_vma=False
    )
```

```python
import jax
import jax.numpy as jnp
from jax import lax
from jax.experimental import pallas as pl
from jax.experimental.pallas import tpu as pltpu
from jax.sharding import PartitionSpec as P

HEADS = 8
TOP = 2


def slot_table(targets, tile_count, capacity):
    tile_ids = jnp.arange(tile_count, dtype=jnp.int32)
    named = jnp.any(targets[:, :, None] == tile_ids[None, None, :], axis=1)
    position = jnp.cumsum(named.astype(jnp.int32), axis=0) - 1
    places = jnp.arange(capacity, dtype=jnp.int32)
    chosen = named.T[:, None, :] & (position.T[:, None, :] == places[None, :, None])
    return (chosen, jnp.sum(named.astype(jnp.int32), axis=0))


def attention_kernel(
    q_ref, g_ref, f_ref, wk_ref, wv_ref, live_ref, x_ref, c_ref,
    o_ref, dq_ref, dk_ref, dv_ref, pieces_ref,
    k_ref, v_ref, dk_acc, dv_acc, pq_ref, pk_ref, pv_ref, po_ref,
):
    step = pl.program_id(0)
    width = q_ref.shape[1]
    head_size = width // HEADS
    factor = head_size ** (-0.5)

    @pl.when(step == 0)
    def _():
        dk_acc[...] = jnp.zeros_like(dk_acc)
        dv_acc[...] = jnp.zeros_like(dv_acc)
        po_ref[...] = jnp.zeros_like(po_ref)
        pq_ref[...] = jnp.zeros_like(pq_ref)
        feat = f_ref[...]
        k_ref[...] = jnp.dot(feat, wk_ref[...], preferred_element_type=jnp.float32).astype(k_ref.dtype)
        v_ref[...] = jnp.dot(feat, wv_ref[...], preferred_element_type=jnp.float32).astype(v_ref.dtype)

    live = live_ref[...] > 0.5
    for h in range(HEADS):
        cols = slice(h * head_size, (h + 1) * head_size)
        q_h = q_ref[:, cols]
        g_h = g_ref[:, cols]
        k_h = k_ref[:, cols]
        v_h = v_ref[:, cols]
        nt = (((1,), (1,)), ((), ()))
        tn = (((0,), (0,)), ((), ()))
        scores = lax.dot_general(q_h, k_h, nt, preferred_element_type=jnp.float32) * factor
        scores = jnp.where(live, scores, -1e30)
        peak = jnp.max(scores, axis=1, keepdims=True)
        raised = jnp.exp(scores - peak)
        attention = raised / jnp.sum(raised, axis=1, keepdims=True)
        prob_half = attention.astype(jnp.bfloat16)
        o_ref[:, cols] = jnp.dot(prob_half, v_h, preferred_element_type=jnp.float32).astype(o_ref.dtype)
        prob_grad = lax.dot_general(g_h, v_h, nt, preferred_element_type=jnp.float32)
        correction = jnp.sum(attention * prob_grad, axis=1, keepdims=True)
        score_grad = (attention * (prob_grad - correction) * factor).astype(jnp.bfloat16)
        dq_ref[:, cols] = jnp.dot(score_grad, k_h, preferred_element_type=jnp.float32).astype(dq_ref.dtype)
        dk_acc[:, cols] += lax.dot_general(score_grad, q_h, tn, preferred_element_type=jnp.float32)
        dv_acc[:, cols] += lax.dot_general(prob_half, g_h, tn, preferred_element_type=jnp.float32)

    tn = (((0,), (0,)), ((), ()))
    po_ref[...] += lax.dot_general(o_ref[...], c_ref[...], tn, preferred_element_type=jnp.float32)
    pq_ref[...] += lax.dot_general(x_ref[...], dq_ref[...], tn, preferred_element_type=jnp.float32)

    @pl.when(step == pl.num_programs(0) - 1)
    def _():
        key_grad = dk_acc[...].astype(dk_ref.dtype)
        value_grad = dv_acc[...].astype(dv_ref.dtype)
        dk_ref[...] = key_grad
        dv_ref[...] = value_grad
        pk_ref[...] = lax.dot_general(f_ref[...], key_grad, tn, preferred_element_type=jnp.float32)
        pv_ref[...] = lax.dot_general(f_ref[...], value_grad, tn, preferred_element_type=jnp.float32)
        parts = (pq_ref, pk_ref, pv_ref, po_ref)
        col_tiles = width // 128
        per_device = (width // 8) * col_tiles // pieces_ref.shape[0]
        depth = 8 * per_device

        def scatter_row(r, carry):
            for c in range(col_tiles):
                tile = r * col_tiles + c
                for i, part in enumerate(parts):
                    pieces_ref[tile // per_device, pl.ds(i * depth + (c % per_device) * 8, 8), :] = (
                        part[pl.ds(r * 8, 8), pl.ds(c * 128, 128)]
                    )
            return carry

        lax.fori_loop(0, width // 8, scatter_row, 0)


def fused_attention(
    queries, out_grad, feat_tile, key_weight, value_weight, live, grid_rows, upstream, count, block=512
):
    rows, width = queries.shape
    slots = feat_tile.shape[0]
    row_block = pl.BlockSpec((block, width), lambda i: (i, 0))
    slot_block = pl.BlockSpec((slots, width), lambda i: (0, 0))
    live_block = pl.BlockSpec((1, slots), lambda i: (0, 0))
    weight_block = pl.BlockSpec((width, width), lambda i: (0, 0))
    depth = 4 * width * width // (count * 128)
    return pl.pallas_call(
        attention_kernel,
        grid=(rows // block,),
        in_specs=[
            row_block, row_block, slot_block, weight_block, weight_block, live_block,
            row_block, row_block,
        ],
        out_specs=[
            row_block, row_block, slot_block, slot_block,
            pl.BlockSpec((count, depth, 128), lambda i: (0, 0, 0)),
        ],
        out_shape=[
            jax.ShapeDtypeStruct((rows, width), jnp.bfloat16),
            jax.ShapeDtypeStruct((rows, width), jnp.bfloat16),
            jax.ShapeDtypeStruct((slots, width), jnp.bfloat16),
            jax.ShapeDtypeStruct((slots, width), jnp.bfloat16),
            jax.ShapeDtypeStruct((count, depth, 128), jnp.float32),
        ],
        scratch_shapes=[
            pltpu.VMEM((slots, width), jnp.bfloat16),
            pltpu.VMEM((slots, width), jnp.bfloat16),
            pltpu.VMEM((slots, width), jnp.float32),
            pltpu.VMEM((slots, width), jnp.float32),
            pltpu.VMEM((width, width), jnp.float32),
            pltpu.VMEM((width, width), jnp.float32),
            pltpu.VMEM((width, width), jnp.float32),
            pltpu.VMEM((width, width), jnp.float32),
        ],
        compiler_params=pltpu.CompilerParams(dimension_semantics=("arbitrary",)),
    )(
        queries, out_grad, feat_tile, key_weight, value_weight,
        live.astype(jnp.float32).reshape(1, slots), grid_rows, upstream,
    )


def send_slots(outgoing):
    arrived = lax.all_to_all(
        outgoing, ("inline", "crosslin"), split_axis=0, concat_axis=0, tiled=True
    )
    return arrived


def from_tiles(tiles, shape):
    return tiles.reshape(shape[0] // 8, shape[1] // 128, 8, 128).transpose(0, 2, 1, 3).reshape(shape)


def sum_over_devices(pieces, shape, rider):
    count = pieces.shape[0]
    depth = pieces.shape[1] // 4
    rider_rows = rider.size // (count * 128)
    blank = jnp.zeros(pieces.shape, jnp.bfloat16)
    payload = jnp.concatenate([blank, rider.reshape(count, rider_rows, 128)], axis=1)
    received, payload = lax.optimization_barrier((send_slots(pieces), payload))
    mine = received.sum(axis=0, keepdims=True).astype(jnp.bfloat16)
    payload = lax.dynamic_update_slice(payload, jnp.broadcast_to(mine, pieces.shape), (0, 0, 0))
    arrived = send_slots(payload)
    gathered = arrived[:, : pieces.shape[1]].astype(jnp.float32)
    sums = tuple(from_tiles(gathered[:, i * depth : (i + 1) * depth], shape) for i in range(4))
    return sums, arrived[:, pieces.shape[1] :].reshape(count * rider_rows, 128)


def on_device(
    grid_feat,
    cotangent,
    trace_feat,
    trace_dest,
    query_weight,
    key_weight,
    value_weight,
    output_weight,
):
    tile_count = lax.axis_size("inline") * lax.axis_size("crosslin")
    trace_rows = trace_feat.shape[0]
    model_width = trace_feat.shape[1]
    capacity = 2 * trace_rows * TOP // tile_count
    chosen, counts = slot_table(trace_dest, tile_count, capacity)
    picker = chosen.astype(jnp.bfloat16).reshape(tile_count * capacity, trace_rows)
    flag = jnp.ones((trace_rows, 128), jnp.bfloat16)
    packed = jnp.concatenate([trace_feat, flag], axis=1)
    outgoing = jnp.dot(picker, packed, preferred_element_type=jnp.float32).astype(jnp.bfloat16)
    arrived = send_slots(outgoing)
    feat_tile = arrived[:, :model_width]
    live_slots = arrived[:, model_width] > 0.5
    queries = jnp.dot(grid_feat, query_weight, preferred_element_type=jnp.float32).astype(
        jnp.bfloat16
    )
    out_grad = jnp.dot(cotangent, output_weight.T, preferred_element_type=jnp.float32).astype(
        jnp.bfloat16
    )
    attn_out, query_grad, key_grad, value_grad, pieces = fused_attention(
        queries, out_grad, feat_tile, key_weight, value_weight, live_slots, grid_feat, cotangent,
        tile_count,
    )
    slot_trace = jnp.dot(key_grad, key_weight.T, preferred_element_type=jnp.float32)
    slot_trace = slot_trace + jnp.dot(
        value_grad, value_weight.T, preferred_element_type=jnp.float32
    )
    (grad_query, grad_key, grad_value, grad_output), returned = sum_over_devices(
        pieces, (model_width, model_width), slot_trace.astype(jnp.bfloat16)
    )
    grad_grid = jnp.dot(query_grad, query_weight.T, preferred_element_type=jnp.float32).astype(
        jnp.bfloat16
    )
    col_blocks = model_width // 128
    spread = picker.reshape(tile_count * capacity, 1, 1, trace_rows) * jnp.eye(
        col_blocks, dtype=picker.dtype
    )[None, :, :, None]
    spread = spread.reshape(tile_count * capacity * col_blocks, col_blocks, trace_rows)
    grad_trace = jnp.einsum(
        "kcr,kl->rcl", spread, returned, preferred_element_type=jnp.float32
    ).reshape(trace_rows, model_width)
    return (grad_grid, grad_trace, grad_query, grad_key, grad_value, grad_output)


def solution(mesh):
    in_specs = (
        P(("inline", "crosslin"), None),
        P(("inline", "crosslin"), None),
        P(("inline", "crosslin"), None),
        P(("inline", "crosslin"), None),
        P(),
        P(),
        P(),
        P(),
    )
    out_specs = (
        P(("inline", "crosslin"), None),
        P(("inline", "crosslin"), None),
        P(),
        P(),
        P(),
        P(),
    )
    return jax.shard_map(
        on_device, mesh=mesh, in_specs=in_specs, out_specs=out_specs, check_vma=False
    )
```
